32 devices in a mesh: dp: 4 (over x, core), fsdp: 8 (over z, y).
Axes of the slice: x: 2, y: 2, z: 4, core: 2. Of those that a mesh axis runs over, the one named last changes fastest.
Arguments:
- tokens: bfloat16 [8192, 640], P(('dp', 'fsdp')), may hold values from -6 to 6
- cotangent: bfloat16 [8192, 640], P(('dp', 'fsdp')), may hold values from -6 to 6
- masked_pos: int32 [8192], P(('dp', 'fsdp')), may hold values from 0 to 1
- labels: int32 [8192], P(('dp', 'fsdp')), may hold values from 0 to 3
- decoder: bfloat16 [4, 640], replicated, may hold values from -0.375 to 0.375
- master: float32 [640, 12800], P('fsdp'), may hold values from -0.6324555 to 0.6324555
- small_params: float32 [640, 16], P('fsdp'), may hold values from -0.8 to 1.4
- small_first: float32 [640, 16], P('fsdp'), may hold values from -128 to 128
- small_second: float32 [640, 16], P('fsdp'), may hold values from 163.84 to 4096
- block_slots: int32 [40], replicated, may hold values from 0 to 39, as said below
- first_moment: float32 [40, 640, 320], P('fsdp'), may hold values from -128 to 128
- second_moment: float32 [40, 640, 320], P('fsdp'), may hold values from 163.84 to 4096
- left_bases: float32 [40, 640, 640], P('fsdp'), may hold values from -1 to 1, as said below
- right_bases: float32 [40, 320, 320], P('fsdp'), may hold values from -1 to 1, as said below
Outputs:
- out_tokens: bfloat16 [8192, 640], P(('dp', 'fsdp'))
- grad_tokens: bfloat16 [8192, 640], P(('dp', 'fsdp'))
- grad_weights: float32 [640, 12800], P('fsdp')
- grad_small: float32 [640, 16], P('fsdp')
- new_first: float32 [40, 640, 320], P('fsdp')
- new_second: float32 [40, 640, 320], P('fsdp')
- new_master: float32 [640, 12800], P('fsdp')
- new_copy: bfloat16 [640, 12800], P('fsdp')
- new_small: float32 [640, 16], P('fsdp')
- new_small_first: float32 [640, 16], P('fsdp')
- new_small_second: float32 [640, 16], P('fsdp')
- loss_accuracy: float32 [5], replicated
- counts: int32 [4], replicated
The draws below stay inside these ranges and needn't reach their ends.
Inputs may be any that keep to these rules, and one draw needn't show every extreme that they name: Distinct slot numbers; block b (columns b * 320 to (b + 1) * 320 - 1 of the weights) keeps its optimizer state in slot block_slots[b], held by fsdp index block_slots[b] // 5; at most 5 blocks on one index. `left_bases`: each slot's matrix is orthogonal. `right_bases`: each slot's matrix is orthogonal.
All inputs are finite; a program needn't handle non-finite values.
Results may differ from the reference program's by a relative error of at most 0.013.
The reference program's roundings to bfloat16 on the way count: a program that leaves them out, or rounds other values in their place, can miss the bound.
Values may be sent and summed in bfloat16 or wider, within the bound.
No kernel may reach another device: no remote copies, remote signals or barrier semaphores. Data moves between devices by JAX's collectives and lax.ppermute only.
A program may use at most 256 MiB of HBM per device.

```python
import math
import jax
import jax.numpy as jnp
from jax import lax

D = 640
HEADS = 20
HEAD_DIM = 32
FF = 5120
SEQ_LEN = 256
NUC = 4
STEP = 5
TOKENS = 8192
SEQS = 32
BW = 320
WCOLS = 12800
BLOCKS = 40
SLOTS = 40
SMALLC = 16


def draw_block_slots(key, part):
    key_pick, key_order = jax.random.split(jax.random.fold_in(key, 11))
    middle_slots = jax.random.permutation(key_pick, SLOTS - 2)[:BLOCKS - 2] + 1
    chosen = jnp.concatenate([jnp.array([0, SLOTS - 1], dtype=jnp.int32), middle_slots.astype(jnp.int32)])
    return chosen[jax.random.permutation(key_order, BLOCKS)].astype(jnp.int32)


def draw_masked_pos(key, part):
    key_rate, key_pick = jax.random.split(jax.random.fold_in(key, 23))
    seq_index = jnp.arange(TOKENS, dtype=jnp.int32) // SEQ_LEN
    jitter = jax.random.randint(key_rate, (SEQS,), 0, 6)
    percent = 10 + 25 * jnp.arange(SEQS, dtype=jnp.int32) // SEQS + jitter
    dice_rolls = jax.random.randint(key_pick, (TOKENS,), 0, 100)
    return (dice_rolls < percent[seq_index]).astype(jnp.int32)


def draw_master(key, part):
    normal_draw = jnp.clip(jax.random.normal(jax.random.fold_in(key, 31), (D, WCOLS), jnp.float32), -4.0, 4.0)
    column = jnp.arange(WCOLS, dtype=jnp.int32)[None, :]
    factor = jnp.where(column < 2 * D, 1.4 / math.sqrt(D), 1.0 / math.sqrt(D))
    factor = jnp.where((column >= 3 * D) & (column < 4 * D), 4.0 / math.sqrt(D), factor)
    factor = jnp.where(column >= 4 * D + FF, 1.0 / math.sqrt(FF), factor)
    return normal_draw * factor


def draw_small_params(key, part):
    normal_draw = jnp.clip(jax.random.normal(jax.random.fold_in(key, 41), (D, SMALLC), jnp.float32), -4.0, 4.0)
    column = jnp.arange(SMALLC, dtype=jnp.int32)[None, :]
    is_gain = (column == 0) | (column == 5)
    return jnp.where(is_gain, 1.0 + 0.1 * normal_draw, 0.2 * normal_draw)


def orthogonal_set(key, matrix_count, matrix_order):
    gaussian = jax.random.normal(key, (matrix_count, matrix_order, matrix_order), jnp.float32)
    q_factor, r_factor = jnp.linalg.qr(gaussian)
    diagonal_r = jnp.diagonal(r_factor, axis1=1, axis2=2)
    column_sign = jnp.where(diagonal_r < 0.0, -1.0, 1.0).astype(jnp.float32)
    return (q_factor * column_sign[:, None, :]).astype(jnp.float32)


def draw_left_bases(key, part):
    return orthogonal_set(jax.random.fold_in(key, 51), SLOTS, D)


def draw_right_bases(key, part):
    return orthogonal_set(jax.random.fold_in(key, 61), SLOTS, BW)


def set_ends(result, own_key, least, high):
    longest = result.shape.index(max(result.shape))
    spots = []
    for shift in (0, 1):
        where = [jax.random.randint(jax.random.fold_in(own_key, axis), (), 0, length) for axis, length in enumerate(result.shape)]
        where[longest] = (where[longest] + shift) % result.shape[longest]
        spots.append(tuple(where))
    return result.at[spots[0]].set(least).at[spots[1]].set(high)


def block_levels(rng, dims, cuts, smallest, high):
    gain = 1.0
    for dim, shards_of in cuts:
        steps = jax.random.uniform(jax.random.fold_in(jax.random.fold_in(rng, 6), dim), (shards_of,), jnp.float32, smallest / len(cuts), high / len(cuts))
        gain = gain * jnp.repeat(jnp.exp(steps), dims[dim] // shards_of).reshape((-1,) + (1,) * (len(dims) - 1 - dim))
    return gain


def bell_draw(rng, shape, width, limit, shards=(), kind=jnp.bfloat16):
    loudness = block_levels(rng, shape, shards, -0.22, 0.18) if shards else 1.0
    drawn = jax.random.normal(rng, shape, jnp.float32) * width * loudness
    return jnp.minimum(jnp.maximum(drawn, -limit), limit).astype(kind)


def setup_inputs(seed: int = 0) -> dict:
    arg_keys = jax.random.split(jax.random.key(seed), 15)
    tokens = bell_draw(arg_keys[0], (TOKENS, D), 1.0, 6.0, ((0, 32),))
    cotangent = bell_draw(arg_keys[1], (TOKENS, D), 1.0, 6.0, ((0, 32),))
    masked_pos = draw_masked_pos(jax.random.fold_in(arg_keys[14], 71), 0)
    labels = set_ends(jax.random.randint(arg_keys[3], (TOKENS,), 0, NUC), jax.random.fold_in(arg_keys[3], 1), 0, NUC - 1).astype(jnp.int32)
    decoder = bell_draw(arg_keys[4], (NUC, D), (1.5 * D ** -0.5), 0.375)
    master = draw_master(jax.random.fold_in(arg_keys[14], 71), 0)
    small_params = draw_small_params(jax.random.fold_in(arg_keys[14], 71), 0)
    small_first = bell_draw(arg_keys[7], (D, SMALLC), (0.25 * TOKENS ** 0.5), 128.0, ((0, 8),), jnp.float32)
    small_second = jnp.clip(jnp.exp(math.log(4096.0) - 3.218876 * jax.random.uniform(arg_keys[8], (D, SMALLC), jnp.float32) ** block_levels(arg_keys[8], (D, SMALLC), ((0, 8),), -0.2, 0.2)), 163.84, 4096.0)
    block_slots = draw_block_slots(jax.random.fold_in(arg_keys[14], 71), 0)
    first_moment = bell_draw(arg_keys[10], (SLOTS, D, BW), (0.25 * TOKENS ** 0.5), 128.0, ((0, 8),), jnp.float32)
    second_moment = jnp.clip(jnp.exp(math.log(4096.0) - 3.218876 * jax.random.uniform(arg_keys[11], (SLOTS, D, BW), jnp.float32) ** block_levels(arg_keys[11], (SLOTS, D, BW), ((0, 8),), -0.2, 0.2)), 163.84, 4096.0)
    left_bases = draw_left_bases(jax.random.fold_in(arg_keys[14], 71), 0)
    right_bases = draw_right_bases(jax.random.fold_in(arg_keys[14], 71), 0)
    return dict(tokens=tokens, cotangent=cotangent, masked_pos=masked_pos, labels=labels, decoder=decoder, master=master, small_params=small_params, small_first=small_first, small_second=small_second, block_slots=block_slots, first_moment=first_moment, second_moment=second_moment, left_bases=left_bases, right_bases=right_bases)


EPS_NORM = 1e-05
EPS_ADAM = 1e-08
BETA_FIRST = 0.5
BETA_SECOND = 0.5
RATE_MATRIX = 0.02
RATE_VECTOR = 0.05
EXACT_PRECISION = lax.Precision.HIGHEST

@jax.custom_vjp
def low(v):
    return lax.optimization_barrier(v.astype(jnp.bfloat16)).astype(jnp.float32)

@jax.custom_vjp
def low_back(v):
    return v

def low_keep(v):
    return (low(v), None)

def low_pass(kept, grad):
    return (grad,)

def back_keep(v):
    return (v, None)

def back_low(kept, grad):
    return (low(grad),)
low.defvjp(low_keep, low_pass)
low_back.defvjp(back_keep, back_low)

def normalize_layer(rows_in, norm_gain, norm_shift):
    centred = rows_in - lax.optimization_barrier(jnp.mean(rows_in, axis=-1, keepdims=True))
    variance = lax.optimization_barrier(jnp.mean(centred * centred, axis=-1, keepdims=True))
    return centred * lax.rsqrt(variance + EPS_NORM) * norm_gain + norm_shift

def adam_direction(first_new, second_new):
    return first_new / (1.0 - BETA_FIRST ** STEP) / (jnp.sqrt(second_new / (1.0 - BETA_SECOND ** STEP)) + EPS_ADAM)

def forward(rows_in, weights, params):
    gain_one, shift_one, bias_query, bias_value, bias_output, gain_two, shift_two, bias_down = [params[:, column] for column in range(8)]
    bias_up = params[:, 8:].reshape(FF)
    inv_root = HEAD_DIM ** (-0.5)
    normed = low(normalize_layer(rows_in, gain_one, shift_one))
    queries = low(low_back(jnp.dot(normed, weights[:, :D], precision=EXACT_PRECISION) + bias_query))
    key_rows = low(low_back(jnp.dot(normed, weights[:, D:2 * D], precision=EXACT_PRECISION)))
    values = low(low_back(jnp.dot(normed, weights[:, 2 * D:3 * D], precision=EXACT_PRECISION) + bias_value))
    shape_heads = (rows_in.shape[0] // SEQ_LEN, SEQ_LEN, HEADS, HEAD_DIM)
    scores = jnp.einsum('slhd,smhd->shlm', queries.reshape(shape_heads), key_rows.reshape(shape_heads), precision=EXACT_PRECISION) * inv_root
    probabilities = low(jax.nn.softmax(low_back(scores), axis=-1))
    mixed_rows = jnp.einsum('shlm,smhd->slhd', probabilities, values.reshape(shape_heads), precision=EXACT_PRECISION).reshape(rows_in.shape[0], D)
    attention_result = low(low_back(mixed_rows))
    middle = rows_in + low_back(jnp.dot(attention_result, weights[:, 3 * D:4 * D], precision=EXACT_PRECISION) + bias_output)
    normed_two = low(normalize_layer(middle, gain_two, shift_two))
    pre_active = low_back(jnp.dot(normed_two, weights[:, 4 * D:4 * D + FF], precision=EXACT_PRECISION) + bias_up)
    active = low(jax.nn.gelu(pre_active, approximate=False))
    return middle + jnp.dot(active, weights[:, 4 * D + FF:].T, precision=EXACT_PRECISION) + bias_down

def reference(tokens, cotangent, masked_pos, labels, decoder, master, small_params, small_first, small_second, block_slots, first_moment, second_moment, left_bases, right_bases):
    weights = low(master)
    params = low(small_params)
    group_rows = min(TOKENS, 4096)
    group_count = TOKENS // group_rows
    rows_all = tokens.astype(jnp.float32).reshape(group_count, group_rows, D)
    back_all = cotangent.astype(jnp.float32).reshape(group_count, group_rows, D)

    def group_step(totals, inputs):
        layer_out, pull_back = jax.vjp(forward, inputs[0], weights, params)
        d_rows, d_weights, d_params = pull_back(inputs[1])
        return ((totals[0] + d_weights, totals[1] + d_params), (layer_out.astype(jnp.bfloat16), d_rows.astype(jnp.bfloat16)))
    zero_totals = (jnp.zeros((D, WCOLS), jnp.float32), jnp.zeros((D, SMALLC), jnp.float32))
    (grad_weights, grad_small), (out_groups, back_groups) = lax.scan(group_step, zero_totals, (rows_all, back_all))
    out_tokens = out_groups.reshape(TOKENS, D)
    grad_tokens = back_groups.reshape(TOKENS, D)
    logits = jnp.dot(out_tokens.astype(jnp.float32), decoder.T.astype(jnp.float32), preferred_element_type=jnp.float32)
    log_norm = jax.nn.logsumexp(logits, axis=-1)
    one_hot = (labels[:, None] == jnp.arange(NUC, dtype=jnp.int32)[None, :]).astype(jnp.float32)
    hidden_tokens = masked_pos.astype(jnp.float32)
    chosen = one_hot * hidden_tokens[:, None]
    entropy = log_norm - lax.optimization_barrier(jnp.sum(one_hot * logits, axis=-1))
    right_prob = lax.optimization_barrier(jnp.sum(one_hot * jnp.exp(logits - log_norm[:, None]), axis=-1))
    loss_sum = jnp.sum(hidden_tokens * entropy)
    prob_sums = lax.optimization_barrier(jnp.sum(chosen * right_prob[:, None], axis=0))
    count_sums = lax.optimization_barrier(jnp.sum(chosen, axis=0))
    loss_accuracy = jnp.concatenate([(loss_sum / jnp.maximum(jnp.sum(count_sums), 1.0))[None], prob_sums / jnp.maximum(count_sums, 1.0)])
    counts = count_sums.astype(jnp.int32)
    weight_blocks = grad_weights.reshape(D, BLOCKS, BW).transpose(1, 0, 2)
    selected_left_bases = left_bases[block_slots]
    right_chosen = right_bases[block_slots]
    eigen_turned = jnp.einsum('asr,asw->arw', selected_left_bases, weight_blocks, precision=EXACT_PRECISION)
    eigen_turned = jnp.einsum('bic,bcj->bij', eigen_turned, right_chosen, precision=EXACT_PRECISION)
    first_new = BETA_FIRST * first_moment[block_slots] + (1.0 - BETA_FIRST) * eigen_turned
    second_new = BETA_SECOND * second_moment[block_slots] + (1.0 - BETA_SECOND) * eigen_turned * eigen_turned
    direction = adam_direction(first_new, second_new)
    rotated_gradient = jnp.einsum('bij,blj->bil', direction, right_chosen, precision=EXACT_PRECISION)
    rotated_gradient = jnp.einsum('yzj,yjm->yzm', selected_left_bases, rotated_gradient, precision=EXACT_PRECISION)
    update = rotated_gradient.transpose(1, 0, 2).reshape(D, WCOLS)
    new_master = master - RATE_MATRIX * update
    new_copy = new_master.astype(jnp.bfloat16)
    new_first = jnp.zeros((SLOTS, D, BW), jnp.float32).at[block_slots].set(first_new)
    new_second = jnp.zeros((SLOTS, D, BW), jnp.float32).at[block_slots].set(second_new)
    new_small_first = BETA_FIRST * small_first + (1.0 - BETA_FIRST) * grad_small
    new_small_second = BETA_SECOND * small_second + (1.0 - BETA_SECOND) * grad_small * grad_small
    new_small = small_params - RATE_VECTOR * adam_direction(new_small_first, new_small_second)
    return (out_tokens, grad_tokens, grad_weights, grad_small, new_first, new_second, new_master, new_copy, new_small, new_small_first, new_small_second, loss_accuracy, counts)
```

```python
import jax
import jax.numpy as jnp
from jax import lax
from jax.sharding import PartitionSpec as P

HEAD_DIM = 32
SEQ_LEN = 256
STEP = 5


EPS_NORM = 1e-05
EPS_ADAM = 1e-08
BETA_FIRST = 0.5
BETA_SECOND = 0.5
RATE_MATRIX = 0.02
RATE_VECTOR = 0.05
EXACT_PRECISION = lax.Precision.HIGHEST


def normalize_layer(rows_in, norm_gain, norm_shift):
    centred = rows_in - jnp.mean(rows_in, axis=-1, keepdims=True)
    variance = jnp.mean(centred * centred, axis=-1, keepdims=True)
    return centred * lax.rsqrt(variance + EPS_NORM) * norm_gain + norm_shift


def exact_gelu(inputs):
    return jax.nn.gelu(inputs, approximate=False)


def adam_direction(first_new, second_new):
    return (
        first_new
        / (1.0 - BETA_FIRST**STEP)
        / (jnp.sqrt(second_new / (1.0 - BETA_SECOND**STEP)) + EPS_ADAM)
    )


def contract_rows(left_mat, right_mat):
    return lax.dot_general(
        left_mat, right_mat, (((0,), (0,)), ((), ())), preferred_element_type=jnp.float32
    )


def times_transpose(left_mat, right_mat):
    return lax.dot_general(
        left_mat, right_mat, (((1,), (1,)), ((), ())), preferred_element_type=jnp.float32
    )


def block_scores(queries, key_rows):
    return jnp.einsum(
        "slhd,smhd->shlm", queries, key_rows, preferred_element_type=jnp.float32
    ) * HEAD_DIM ** (-0.5)


def attend_block(weight_blocks):
    queries, key_rows, values = weight_blocks
    scores = block_scores(queries, key_rows)
    highest = jnp.max(scores, axis=-1, keepdims=True)
    exponent = jnp.exp(scores - highest)
    totals = jnp.sum(exponent, axis=-1, keepdims=True)
    weights_soft = (exponent / totals).astype(jnp.bfloat16)
    mixed_rows = jnp.einsum(
        "shlm,smhd->slhd", weights_soft, values, preferred_element_type=jnp.float32
    )
    return (mixed_rows.astype(jnp.bfloat16), (highest + jnp.log(totals))[..., 0])


def attend_back(weight_blocks):
    queries, key_rows, values, log_total, d_attended = weight_blocks
    probabilities = jnp.exp(block_scores(queries, key_rows) - log_total[..., None])
    d_values = jnp.einsum(
        "shlm,slhd->smhd",
        probabilities.astype(jnp.bfloat16),
        d_attended,
        preferred_element_type=jnp.float32,
    )
    d_probs = jnp.einsum("slhd,smhd->shlm", d_attended, values, preferred_element_type=jnp.float32)
    d_scores = (
        probabilities * (d_probs - jnp.sum(probabilities * d_probs, axis=-1, keepdims=True))
    ).astype(jnp.bfloat16)
    d_queries = jnp.einsum(
        "shlm,smhd->slhd", d_scores, key_rows, preferred_element_type=jnp.float32
    ) * HEAD_DIM ** (-0.5)
    d_keys = jnp.einsum(
        "shlm,slhd->smhd", d_scores, queries, preferred_element_type=jnp.float32
    ) * HEAD_DIM ** (-0.5)
    return (
        d_queries.astype(jnp.bfloat16),
        d_keys.astype(jnp.bfloat16),
        d_values.astype(jnp.bfloat16),
    )


def local(
    tokens,
    cotangent,
    masked_pos,
    labels,
    decoder,
    master,
    small_params,
    small_first,
    small_second,
    block_slots,
    first_moment,
    second_moment,
    left_bases,
    right_bases,
):
    model_width = decoder.shape[1]
    hidden = (master.shape[1] - 4 * model_width) // 2
    heads_count = model_width // HEAD_DIM
    token_count = tokens.shape[0]
    weight_cols = master.shape[1]
    packed_local = jnp.concatenate(
        [master.astype(jnp.bfloat16), small_params.astype(jnp.bfloat16)], axis=1
    )
    packed = lax.all_gather(packed_local, "fsdp", axis=0, tiled=True)
    weights = packed[:, :weight_cols]
    params = packed[:, weight_cols:].astype(jnp.float32)
    gain_one, shift_one, bias_query, bias_value, bias_output, gain_two, shift_two, bias_down = [
        params[:, column] for column in range(8)
    ]
    bias_up = params[:, 8:].reshape(hidden)
    rows_in = tokens.astype(jnp.float32)
    normed = normalize_layer(rows_in, gain_one, shift_one).astype(jnp.bfloat16)
    bias_qkv = jnp.concatenate([bias_query, jnp.zeros_like(bias_query), bias_value])
    projected = (
        jnp.dot(normed, weights[:, : 3 * model_width], preferred_element_type=jnp.float32)
        + bias_qkv
    ).astype(jnp.bfloat16)
    seq_count = token_count // SEQ_LEN
    per_block = max(1, min(seq_count, 512 // SEQ_LEN))
    block_shape = (seq_count // per_block, per_block, SEQ_LEN, heads_count, HEAD_DIM)
    queries = projected[:, :model_width].reshape(block_shape)
    key_rows = projected[:, model_width : 2 * model_width].reshape(block_shape)
    values = projected[:, 2 * model_width :].reshape(block_shape)
    attention_result, log_total = lax.map(attend_block, (queries, key_rows, values))
    attention_result = attention_result.reshape(token_count, model_width)
    middle = (
        rows_in
        + jnp.dot(
            attention_result,
            weights[:, 3 * model_width : 4 * model_width],
            preferred_element_type=jnp.float32,
        )
        + bias_output
    )
    normed_two = normalize_layer(middle, gain_two, shift_two).astype(jnp.bfloat16)
    pre_active = (
        jnp.dot(
            normed_two,
            weights[:, 4 * model_width : 4 * model_width + hidden],
            preferred_element_type=jnp.float32,
        )
        + bias_up
    )
    active = exact_gelu(pre_active).astype(jnp.bfloat16)
    output_rows = (
        middle + times_transpose(active, weights[:, 4 * model_width + hidden :]) + bias_down
    )
    out_tokens = output_rows.astype(jnp.bfloat16)
    logits = times_transpose(out_tokens, decoder)
    log_norm = jax.nn.logsumexp(logits, axis=-1)
    one_hot = (labels[:, None] == jnp.arange(decoder.shape[0], dtype=jnp.int32)[None, :]).astype(
        jnp.float32
    )
    hidden_tokens = masked_pos.astype(jnp.float32)
    chosen = one_hot * hidden_tokens[:, None]
    entropy = log_norm - jnp.sum(one_hot * logits, axis=-1)
    right_prob = jnp.sum(one_hot * jnp.exp(logits - log_norm[:, None]), axis=-1)
    local_sums = jnp.concatenate(
        [jnp.sum(hidden_tokens * entropy)[None], jnp.sum(chosen * right_prob[:, None], axis=0)]
    )
    global_sums, global_counts = lax.psum((local_sums, jnp.sum(chosen, axis=0)), ("dp", "fsdp"))
    loss_accuracy = jnp.concatenate(
        [
            global_sums[:1] / jnp.maximum(jnp.sum(global_counts), 1.0),
            global_sums[1:] / jnp.maximum(global_counts, 1.0),
        ]
    )
    counts = global_counts.astype(jnp.int32)
    weights_back = weights
    params_back = params
    back_rows = cotangent.astype(jnp.float32)
    d_active = jnp.dot(
        cotangent, weights_back[:, 4 * model_width + hidden :], preferred_element_type=jnp.float32
    )
    unused, gelu_pull = jax.vjp(exact_gelu, pre_active)
    d_pre = gelu_pull(d_active)[0].astype(jnp.bfloat16)
    d_normed_two = times_transpose(
        d_pre, weights_back[:, 4 * model_width : 4 * model_width + hidden]
    )
    unused, norm_pull_two = jax.vjp(normalize_layer, middle, params_back[:, 5], params_back[:, 6])
    d_middle_norm, d_gain_two, d_shift_two = norm_pull_two(d_normed_two)
    d_middle = back_rows + d_middle_norm
    d_branch = d_middle.astype(jnp.bfloat16)
    d_attended = times_transpose(
        d_branch, weights_back[:, 3 * model_width : 4 * model_width]
    ).astype(jnp.bfloat16)
    d_queries, d_keys, d_values = lax.map(
        attend_back, (queries, key_rows, values, log_total, d_attended.reshape(block_shape))
    )
    d_projected = jnp.concatenate(
        [
            d_queries.reshape(token_count, model_width),
            d_keys.reshape(token_count, model_width),
            d_values.reshape(token_count, model_width),
        ],
        axis=1,
    )
    d_normed = times_transpose(d_projected, weights_back[:, : 3 * model_width])
    unused, norm_pull_one = jax.vjp(normalize_layer, rows_in, params_back[:, 0], params_back[:, 1])
    d_rows_norm, d_gain_one, d_shift_one = norm_pull_one(d_normed)
    grad_tokens = (d_middle + d_rows_norm).astype(jnp.bfloat16)
    grad_w_local = jnp.concatenate(
        [
            contract_rows(normed, d_projected),
            contract_rows(attention_result, d_branch),
            contract_rows(normed_two, d_pre),
            contract_rows(cotangent, active),
        ],
        axis=1,
    )
    proj_sums = jnp.sum(d_projected.astype(jnp.float32), axis=0)
    small_cols = jnp.stack(
        [
            d_gain_one,
            d_shift_one,
            proj_sums[:model_width],
            proj_sums[2 * model_width :],
            jnp.sum(d_branch.astype(jnp.float32), axis=0),
            d_gain_two,
            d_shift_two,
            jnp.sum(back_rows, axis=0),
        ],
        axis=1,
    )
    grad_s_local = jnp.concatenate(
        [small_cols, jnp.sum(d_pre.astype(jnp.float32), axis=0).reshape(model_width, -1)], axis=1
    )
    replicas = lax.axis_size("dp")
    small_cols = grad_s_local.shape[1]
    chunk_w = weight_cols // replicas
    chunk_s = small_cols // replicas
    pad_s = 128 - chunk_s
    joined = jnp.concatenate(
        [
            grad_w_local.reshape(-1, replicas, chunk_w),
            grad_s_local.reshape(-1, replicas, chunk_s),
            jnp.zeros((grad_w_local.shape[0], replicas, pad_s), jnp.float32),
        ],
        axis=2,
    ).reshape(grad_w_local.shape[0], -1).astype(jnp.bfloat16)
    joined = lax.psum_scatter(joined, "dp", scatter_dimension=1, tiled=True)
    joined = lax.psum_scatter(joined, "fsdp", scatter_dimension=0, tiled=True)
    joined = lax.all_gather(joined, "dp", axis=1, tiled=True).astype(jnp.float32)
    joined = joined.reshape(joined.shape[0], replicas, chunk_w + chunk_s + pad_s)
    grad_w = joined[:, :, :chunk_w].reshape(joined.shape[0], weight_cols)
    grad_s = joined[:, :, chunk_w : chunk_w + chunk_s].reshape(joined.shape[0], small_cols)
    row_count = grad_w.shape[0]
    block_width = model_width // 2
    block_count = grad_w.shape[1] // block_width
    owned_slots = first_moment.shape[0]
    devices = lax.axis_size("fsdp")
    slot_ids = jnp.arange(owned_slots * devices, dtype=jnp.int32)
    matches = block_slots[None, :] == slot_ids[:, None]
    in_use = jnp.any(matches, axis=1)
    source_block = jnp.sum(
        jnp.where(matches, jnp.arange(block_count, dtype=jnp.int32)[None, :], 0), axis=1
    )
    outgoing = jnp.take(grad_w.reshape(row_count, block_count, block_width), source_block, axis=1)
    outgoing = jnp.where(in_use[None, :, None], outgoing, 0.0).reshape(
        row_count, devices, owned_slots, block_width
    )
    incoming = lax.all_to_all(
        outgoing.astype(jnp.bfloat16), "fsdp", split_axis=1, concat_axis=0, tiled=True
    ).reshape(row_count * devices, owned_slots, block_width).astype(jnp.float32)
    my_use = lax.dynamic_slice_in_dim(in_use, lax.axis_index("fsdp") * owned_slots, owned_slots)
    eigen_turned = jnp.einsum("kdi,dkc->kic", left_bases, incoming, precision=EXACT_PRECISION)
    eigen_turned = jnp.einsum("kic,kcj->kij", eigen_turned, right_bases, precision=EXACT_PRECISION)
    first_new = BETA_FIRST * first_moment + (1.0 - BETA_FIRST) * eigen_turned
    second_new = BETA_SECOND * second_moment + (1.0 - BETA_SECOND) * eigen_turned * eigen_turned
    direction = adam_direction(first_new, second_new)
    rotated_gradient = jnp.einsum("kij,klj->kil", direction, right_bases, precision=EXACT_PRECISION)
    rotated_gradient = jnp.einsum(
        "kdi,kil->dkl", left_bases, rotated_gradient, precision=EXACT_PRECISION
    )
    returned = lax.all_to_all(
        rotated_gradient.reshape(devices, row_count, owned_slots, block_width).astype(
            jnp.bfloat16
        ),
        "fsdp",
        split_axis=0,
        concat_axis=0,
        tiled=True,
    ).astype(jnp.float32)
    by_slot = jnp.moveaxis(returned, 1, 0).reshape(row_count, devices * owned_slots, block_width)
    update = jnp.take(by_slot, block_slots, axis=1).reshape(row_count, block_count * block_width)
    new_master = master - RATE_MATRIX * update
    new_copy = new_master.astype(jnp.bfloat16)
    keep_slot = my_use[:, None, None]
    new_first = jnp.where(keep_slot, first_new, 0.0)
    new_second = jnp.where(keep_slot, second_new, 0.0)
    new_small_first = BETA_FIRST * small_first + (1.0 - BETA_FIRST) * grad_s
    new_small_second = BETA_SECOND * small_second + (1.0 - BETA_SECOND) * grad_s * grad_s
    new_small = small_params - RATE_VECTOR * adam_direction(new_small_first, new_small_second)
    return (
        out_tokens,
        grad_tokens,
        grad_w,
        grad_s,
        new_first,
        new_second,
        new_master,
        new_copy,
        new_small,
        new_small_first,
        new_small_second,
        loss_accuracy,
        counts,
    )


def solution(mesh):
    return jax.shard_map(
        local,
        mesh=mesh,
        in_specs=(
            P(("dp", "fsdp"), None),
            P(("dp", "fsdp"), None),
            P(("dp", "fsdp")),
            P(("dp", "fsdp")),
            P(),
            P("fsdp", None),
            P("fsdp", None),
            P("fsdp", None),
            P("fsdp", None),
            P(),
            P("fsdp", None, None),
            P("fsdp", None, None),
            P("fsdp", None, None),
            P("fsdp", None, None),
        ),
        out_specs=(
            P(("dp", "fsdp"), None),
            P(("dp", "fsdp"), None),
            P("fsdp", None),
            P("fsdp", None),
            P("fsdp", None, None),
            P("fsdp", None, None),
            P("fsdp", None),
            P("fsdp", None),
            P("fsdp", None),
            P("fsdp", None),
            P("fsdp", None),
            P(),
            P(),
        ),
        check_vma=False,
    )
```

```python
import jax
import jax.numpy as jnp
from jax import lax
from jax.sharding import PartitionSpec as P

HEAD_DIM = 32
SEQ_LEN = 256
STEP = 5
LANE = 128


EPS_NORM = 1e-05
EPS_ADAM = 1e-08
BETA_FIRST = 0.5
BETA_SECOND = 0.5
RATE_MATRIX = 0.02
RATE_VECTOR = 0.05
EXACT_PRECISION = lax.Precision.HIGHEST
OPT_PRECISION = lax.Precision.HIGH


def normalize_layer(rows_in, norm_gain, norm_shift):
    centred = rows_in - jnp.mean(rows_in, axis=-1, keepdims=True)
    variance = jnp.mean(centred * centred, axis=-1, keepdims=True)
    return centred * lax.rsqrt(variance + EPS_NORM) * norm_gain + norm_shift


def exact_gelu(inputs):
    return jax.nn.gelu(inputs, approximate=False)


def adam_direction(first_new, second_new):
    return (
        first_new
        / (1.0 - BETA_FIRST**STEP)
        / (jnp.sqrt(second_new / (1.0 - BETA_SECOND**STEP)) + EPS_ADAM)
    )


def contract_rows(left_mat, right_mat):
    return jnp.dot(left_mat.T, right_mat, preferred_element_type=jnp.float32)


def times_transpose(left_mat, right_mat):
    return lax.dot_general(
        left_mat, right_mat, (((1,), (1,)), ((), ())), preferred_element_type=jnp.float32
    )


def block_scores(queries, key_rows):
    return jnp.einsum(
        "slhd,smhd->shlm", queries, key_rows, preferred_element_type=jnp.float32
    ) * HEAD_DIM ** (-0.5)


def attend_block(weight_blocks):
    queries, key_rows, values = weight_blocks
    scores = block_scores(queries, key_rows)
    highest = jnp.max(scores, axis=-1, keepdims=True)
    exponent = jnp.exp(scores - highest)
    totals = jnp.sum(exponent, axis=-1, keepdims=True)
    weights_soft = (exponent / totals).astype(jnp.bfloat16)
    mixed_rows = jnp.einsum(
        "shlm,smhd->slhd", weights_soft, values, preferred_element_type=jnp.float32
    )
    return (mixed_rows.astype(jnp.bfloat16), (highest + jnp.log(totals))[..., 0])


def attend_back(weight_blocks):
    queries, key_rows, values, log_total, d_attended = weight_blocks
    probabilities = jnp.exp(block_scores(queries, key_rows) - log_total[..., None])
    d_values = jnp.einsum(
        "shlm,slhd->smhd",
        probabilities.astype(jnp.bfloat16),
        d_attended,
        preferred_element_type=jnp.float32,
    )
    d_probs = jnp.einsum("slhd,smhd->shlm", d_attended, values, preferred_element_type=jnp.float32)
    d_scores = (
        probabilities * (d_probs - jnp.sum(probabilities * d_probs, axis=-1, keepdims=True))
    ).astype(jnp.bfloat16)
    d_queries = jnp.einsum(
        "shlm,smhd->slhd", d_scores, key_rows, preferred_element_type=jnp.float32
    ) * HEAD_DIM ** (-0.5)
    d_keys = jnp.einsum(
        "shlm,slhd->smhd", d_scores, queries, preferred_element_type=jnp.float32
    ) * HEAD_DIM ** (-0.5)
    return (
        d_queries.astype(jnp.bfloat16),
        d_keys.astype(jnp.bfloat16),
        d_values.astype(jnp.bfloat16),
    )


def ring_order(coords):
    count = len(coords)
    if count <= 2 or coords[0] is None:
        return list(range(count))

    def near(a, b):
        return sum(abs(p - q) for p, q in zip(coords[a], coords[b])) == 1

    links = [[b for b in range(count) if near(a, b)] for a in range(count)]
    path, seen, budget = [0], {0}, [20000]

    def extend():
        budget[0] -= 1
        if budget[0] < 0:
            return False
        if len(path) == count:
            return near(path[-1], path[0])
        options = [b for b in links[path[-1]] if b not in seen]
        options.sort(key=lambda b: sum(1 for q in links[b] if q not in seen))
        for b in options:
            path.append(b)
            seen.add(b)
            if extend():
                return True
            path.pop()
            seen.discard(b)
        return False

    return path if extend() else list(range(count))


class Ring:
    def __init__(self, order):
        self.order = order
        self.count = len(order)
        self.forward = [(order[p], order[(p + 1) % self.count]) for p in range(self.count)]
        self.backward = [(order[p], order[(p - 1) % self.count]) for p in range(self.count)]
        position = [0] * self.count
        for p, member in enumerate(order):
            position[member] = p
        self.position = position

    def sources(self):
        me = jnp.asarray(self.position, jnp.int32)[lax.axis_index("fsdp")]
        steps = jnp.arange(self.count, dtype=jnp.int32)
        return jnp.asarray(self.order, jnp.int32)[(me - steps) % self.count]

    def chains(self, width, parts):
        cuts = [round(width * i / (2 * parts) / LANE) * LANE for i in range(2 * parts + 1)]
        cuts[-1] = width
        return [(cuts[i], cuts[i + 1], i % 2 == 0) for i in range(2 * parts)]

    def all_gather(self, local, core, side, core_pairs, parts):
        count = self.count
        mine_cols = lax.dynamic_slice_in_dim(local, core * side, side, axis=1)
        other_cols = lax.dynamic_slice_in_dim(local, (1 - core) * side, side, axis=1)
        mine_parts, other_parts = [], []
        for lo, hi, ahead in self.chains(side, parts):
            pairs = self.forward if ahead else self.backward
            piece = mine_cols[:, lo:hi]
            got, passed = [None] * count, [None] * count
            got[0], passed[0] = piece, other_cols[:, lo:hi]
            for step in range(1, count):
                piece = lax.ppermute(piece, "fsdp", pairs)
                k = step if ahead else count - step
                got[k] = piece
                passed[k] = lax.ppermute(piece, "dp", core_pairs)
            mine_parts.append(jnp.concatenate(got, axis=0))
            other_parts.append(jnp.concatenate(passed, axis=0))
        return jnp.concatenate(mine_parts, axis=1), jnp.concatenate(other_parts, axis=1)

    def reduce_scatter(self, full, rows, outer_pairs, core_pairs, parts):
        count = self.count
        width = full.shape[1]
        outs, partners = [], []
        for lo, hi, ahead in self.chains(width, parts):
            pairs = self.forward if ahead else self.backward

            def block(k):
                return full[k * rows : (k + 1) * rows, lo:hi]

            acc = block(1 % count if ahead else count - 1)
            for step in range(1, count):
                got = lax.ppermute(acc.astype(jnp.bfloat16), "fsdp", pairs)
                k = (step + 1) % count if ahead else (count - step - 1) % count
                acc = got.astype(jnp.float32) + block(k)
            other = lax.ppermute(acc.astype(jnp.bfloat16), "dp", outer_pairs)
            acc = acc + other.astype(jnp.float32)
            outs.append(acc)
            partners.append(lax.ppermute(acc, "dp", core_pairs))
        return jnp.concatenate(outs, axis=1), jnp.concatenate(partners, axis=1)


def make_local(ring):
    def local(
        tokens,
        cotangent,
        masked_pos,
        labels,
        decoder,
        master,
        small_params,
        small_first,
        small_second,
        block_slots,
        first_moment,
        second_moment,
        left_bases,
        right_bases,
    ):
        model_width = decoder.shape[1]
        hidden = (master.shape[1] - 4 * model_width) // 2
        heads_count = model_width // HEAD_DIM
        token_count = tokens.shape[0]
        row_count, weight_cols = master.shape
        small_cols = small_params.shape[1]
        members = lax.axis_size("fsdp")
        core = lax.axis_index("dp") % 2
        replicas = lax.axis_size("dp")
        core_pairs = [(i, i ^ 1) for i in range(replicas)]
        outer_pairs = [(i, i ^ 2) for i in range(replicas)]
        half = weight_cols // 2
        lead = LANE
        side = half + lead
        split = (side // LANE + 1) // 2 * LANE

        sources = ring.sources()
        feature_of = (
            sources[:, None] * row_count + jnp.arange(row_count, dtype=jnp.int32)[None, :]
        ).reshape(-1)
        natural_of = jnp.zeros_like(feature_of).at[feature_of].set(
            jnp.arange(feature_of.shape[0], dtype=jnp.int32)
        )

        picker = (
            jnp.arange(model_width, dtype=jnp.int32)[:, None] == feature_of[None, :]
        ).astype(jnp.bfloat16)

        def to_rel(a):
            return jnp.dot(a, picker, preferred_element_type=jnp.float32).astype(a.dtype)

        def to_nat(a):
            return lax.dot_general(
                a, picker, (((1,), (1,)), ((), ())), precision=EXACT_PRECISION,
                preferred_element_type=jnp.float32,
            )

        w_low = master.astype(jnp.bfloat16)
        s_low = small_params.astype(jnp.bfloat16)
        packed_local = jnp.concatenate(
            [
                s_low,
                jnp.zeros((row_count, lead - small_cols), jnp.bfloat16),
                w_low,
                jnp.zeros((row_count, lead), jnp.bfloat16),
            ],
            axis=1,
        )
        mine, other = ring.all_gather(packed_local, core, side, core_pairs, 1)
        full = lax.cond(
            core == 0,
            lambda a, b: jnp.concatenate([a, b], axis=1),
            lambda a, b: jnp.concatenate([b, a], axis=1),
            mine,
            other,
        )
        weights = full[:, lead : lead + weight_cols]
        params = jnp.take(full[:, :small_cols].astype(jnp.float32), natural_of, axis=0)

        gain_one, shift_one, bias_query, bias_value, bias_output, gain_two, shift_two, bias_down = [
            params[:, column] for column in range(8)
        ]
        bias_up = params[:, 8:].reshape(hidden)
        rows_in = tokens.astype(jnp.float32)
        normed = normalize_layer(rows_in, gain_one, shift_one).astype(jnp.bfloat16)
        normed_rel = to_rel(normed)
        bias_qkv = jnp.concatenate([bias_query, jnp.zeros_like(bias_query), bias_value])
        projected = (
            jnp.dot(normed_rel, weights[:, : 3 * model_width], preferred_element_type=jnp.float32)
            + bias_qkv
        ).astype(jnp.bfloat16)
        seq_count = token_count // SEQ_LEN
        per_block = max(1, min(seq_count, 512 // SEQ_LEN))
        block_shape = (seq_count // per_block, per_block, SEQ_LEN, heads_count, HEAD_DIM)
        queries = projected[:, :model_width].reshape(block_shape)
        key_rows = projected[:, model_width : 2 * model_width].reshape(block_shape)
        values = projected[:, 2 * model_width :].reshape(block_shape)
        attention_result, log_total = lax.map(attend_block, (queries, key_rows, values))
        attention_result = attention_result.reshape(token_count, model_width)
        attended_rel = to_rel(attention_result)
        middle = (
            rows_in
            + jnp.dot(
                attended_rel,
                weights[:, 3 * model_width : 4 * model_width],
                preferred_element_type=jnp.float32,
            )
            + bias_output
        )
        normed_two = normalize_layer(middle, gain_two, shift_two).astype(jnp.bfloat16)
        normed_two_rel = to_rel(normed_two)
        pre_active = (
            jnp.dot(
                normed_two_rel,
                weights[:, 4 * model_width : 4 * model_width + hidden],
                preferred_element_type=jnp.float32,
            )
            + bias_up
        )
        active = exact_gelu(pre_active).astype(jnp.bfloat16)
        output_rows = (
            middle
            + to_nat(times_transpose(active, weights[:, 4 * model_width + hidden :]))
            + bias_down
        )
        out_tokens = output_rows.astype(jnp.bfloat16)
        logits = times_transpose(out_tokens, decoder)
        log_norm = jax.nn.logsumexp(logits, axis=-1)
        one_hot = (
            labels[:, None] == jnp.arange(decoder.shape[0], dtype=jnp.int32)[None, :]
        ).astype(jnp.float32)
        hidden_tokens = masked_pos.astype(jnp.float32)
        chosen = one_hot * hidden_tokens[:, None]
        entropy = log_norm - jnp.sum(one_hot * logits, axis=-1)
        right_prob = jnp.sum(one_hot * jnp.exp(logits - log_norm[:, None]), axis=-1)
        local_sums = jnp.concatenate(
            [jnp.sum(hidden_tokens * entropy)[None], jnp.sum(chosen * right_prob[:, None], axis=0)]
        )
        totals = jnp.concatenate([local_sums, jnp.sum(chosen, axis=0)])
        for axis in ("dp", "fsdp"):
            size = lax.axis_size(axis)
            reach = 1
            while reach < size:
                totals = totals + lax.ppermute(
                    totals, axis, [(i, i ^ reach) for i in range(size)]
                )
                reach *= 2
        global_sums, global_counts = totals[: local_sums.shape[0]], totals[local_sums.shape[0] :]
        loss_accuracy = jnp.concatenate(
            [
                global_sums[:1] / jnp.maximum(jnp.sum(global_counts), 1.0),
                global_sums[1:] / jnp.maximum(global_counts, 1.0),
            ]
        )
        counts = global_counts.astype(jnp.int32)
        back_rows = cotangent.astype(jnp.float32)
        cotangent_rel = to_rel(cotangent)
        d_active = jnp.dot(
            cotangent_rel, weights[:, 4 * model_width + hidden :], preferred_element_type=jnp.float32
        )
        unused, gelu_pull = jax.vjp(exact_gelu, pre_active)
        d_pre = gelu_pull(d_active)[0].astype(jnp.bfloat16)
        d_normed_two = to_nat(
            times_transpose(d_pre, weights[:, 4 * model_width : 4 * model_width + hidden])
        )
        unused, norm_pull_two = jax.vjp(normalize_layer, middle, params[:, 5], params[:, 6])
        d_middle_norm, d_gain_two, d_shift_two = norm_pull_two(d_normed_two)
        d_middle = back_rows + d_middle_norm
        d_branch = d_middle.astype(jnp.bfloat16)
        d_attended = to_nat(
            times_transpose(d_branch, weights[:, 3 * model_width : 4 * model_width])
        ).astype(jnp.bfloat16)
        d_queries, d_keys, d_values = lax.map(
            attend_back, (queries, key_rows, values, log_total, d_attended.reshape(block_shape))
        )
        d_projected = jnp.concatenate(
            [
                d_queries.reshape(token_count, model_width),
                d_keys.reshape(token_count, model_width),
                d_values.reshape(token_count, model_width),
            ],
            axis=1,
        )
        d_normed = to_nat(times_transpose(d_projected, weights[:, : 3 * model_width]))
        unused, norm_pull_one = jax.vjp(normalize_layer, rows_in, params[:, 0], params[:, 1])
        d_rows_norm, d_gain_one, d_shift_one = norm_pull_one(d_normed)
        grad_tokens = (d_middle + d_rows_norm).astype(jnp.bfloat16)
        proj_sums = jnp.sum(d_projected.astype(jnp.float32), axis=0)
        small_grads = jnp.stack(
            [
                d_gain_one,
                d_shift_one,
                proj_sums[:model_width],
                proj_sums[2 * model_width :],
                jnp.sum(d_branch.astype(jnp.float32), axis=0),
                d_gain_two,
                d_shift_two,
                jnp.sum(back_rows, axis=0),
            ],
            axis=1,
        )
        small_grads = jnp.concatenate(
            [small_grads, jnp.sum(d_pre.astype(jnp.float32), axis=0).reshape(model_width, -1)], axis=1
        )
        grad_dev = jnp.concatenate(
            [
                jnp.take(small_grads, feature_of, axis=0),
                jnp.zeros((model_width, lead - small_cols), jnp.float32),
                contract_rows(normed_rel, d_projected),
                contract_rows(attended_rel, d_branch),
                contract_rows(normed_two_rel, d_pre),
                contract_rows(cotangent_rel, active),
                jnp.zeros((model_width, lead), jnp.float32),
            ],
            axis=1,
        )
        keep = lax.dynamic_slice_in_dim(grad_dev, core * side, side, axis=1)
        send = lax.dynamic_slice_in_dim(grad_dev, (1 - core) * side, side, axis=1)
        chip = keep + lax.ppermute(send.astype(jnp.bfloat16), "dp", core_pairs).astype(jnp.float32)
        total, partner = ring.reduce_scatter(chip, row_count, outer_pairs, core_pairs, 2)
        joined = lax.cond(
            core == 0,
            lambda a, b: jnp.concatenate([a, b], axis=1),
            lambda a, b: jnp.concatenate([b, a], axis=1),
            total,
            partner,
        )
        grad_w = joined[:, lead : lead + weight_cols]
        grad_s = joined[:, :small_cols]

        block_width = model_width // 2
        block_count = grad_w.shape[1] // block_width
        owned_slots = first_moment.shape[0]
        devices = members
        slot_ids = jnp.arange(owned_slots * devices, dtype=jnp.int32)
        matches = block_slots[None, :] == slot_ids[:, None]
        in_use = jnp.any(matches, axis=1)
        source_block = jnp.sum(
            jnp.where(matches, jnp.arange(block_count, dtype=jnp.int32)[None, :], 0), axis=1
        )
        quarter = block_width // 2
        outgoing = jnp.take(grad_w.reshape(row_count, block_count, block_width), source_block, axis=1)
        outgoing = lax.dynamic_slice_in_dim(outgoing, core * quarter, quarter, axis=2)
        outgoing = jnp.where(in_use[None, :, None], outgoing, 0.0).reshape(
            row_count, devices, owned_slots, quarter
        )
        incoming = lax.all_to_all(
            outgoing.astype(jnp.bfloat16), "fsdp", split_axis=1, concat_axis=0, tiled=True
        ).reshape(row_count * devices, owned_slots, quarter)
        incoming_other = lax.ppermute(incoming, "dp", core_pairs)
        incoming_full = jnp.zeros((row_count * devices, owned_slots, block_width), jnp.bfloat16)
        incoming_full = lax.dynamic_update_slice(incoming_full, incoming, (0, 0, core * quarter))
        incoming_full = lax.dynamic_update_slice(
            incoming_full, incoming_other, (0, 0, (1 - core) * quarter)
        )
        incoming = incoming_full.astype(jnp.float32)
        my_use = lax.dynamic_slice_in_dim(in_use, lax.axis_index("fsdp") * owned_slots, owned_slots)
        eigen_turned = jnp.einsum("kdi,dkc->kic", left_bases, incoming, precision=OPT_PRECISION)
        eigen_turned = jnp.einsum("kic,kcj->kij", eigen_turned, right_bases, precision=OPT_PRECISION)
        first_new = BETA_FIRST * first_moment + (1.0 - BETA_FIRST) * eigen_turned
        second_new = BETA_SECOND * second_moment + (1.0 - BETA_SECOND) * eigen_turned * eigen_turned
        direction = adam_direction(first_new, second_new)
        rotated_gradient = jnp.einsum("kij,klj->kil", direction, right_bases, precision=OPT_PRECISION)
        rotated_gradient = jnp.einsum(
            "kdi,kil->dkl", left_bases, rotated_gradient, precision=OPT_PRECISION
        )
        going = lax.dynamic_slice_in_dim(rotated_gradient, core * quarter, quarter, axis=2)
        returned = lax.all_to_all(
            going.reshape(devices, row_count, owned_slots, quarter).astype(jnp.bfloat16),
            "fsdp",
            split_axis=0,
            concat_axis=0,
            tiled=True,
        )
        returned_other = lax.ppermute(returned, "dp", core_pairs)
        returned_full = jnp.zeros((devices, row_count, owned_slots, block_width), jnp.bfloat16)
        returned_full = lax.dynamic_update_slice(returned_full, returned, (0, 0, 0, core * quarter))
        returned_full = lax.dynamic_update_slice(
            returned_full, returned_other, (0, 0, 0, (1 - core) * quarter)
        )
        owner_of = block_slots // owned_slots
        slot_in = block_slots % owned_slots
        update = returned_full[owner_of, :, slot_in, :].astype(jnp.float32)
        update = jnp.transpose(update, (1, 0, 2)).reshape(row_count, block_count * block_width)
        new_master = master - RATE_MATRIX * update
        new_copy = new_master.astype(jnp.bfloat16)
        keep_slot = my_use[:, None, None]
        new_first = jnp.where(keep_slot, first_new, 0.0)
        new_second = jnp.where(keep_slot, second_new, 0.0)
        new_small_first = BETA_FIRST * small_first + (1.0 - BETA_FIRST) * grad_s
        new_small_second = BETA_SECOND * small_second + (1.0 - BETA_SECOND) * grad_s * grad_s
        new_small = small_params - RATE_VECTOR * adam_direction(new_small_first, new_small_second)
        return (
            out_tokens,
            grad_tokens,
            grad_w,
            grad_s,
            new_first,
            new_second,
            new_master,
            new_copy,
            new_small,
            new_small_first,
            new_small_second,
            loss_accuracy,
            counts,
        )

    return local


def solution(mesh):
    members = mesh.devices[0]
    coords = [tuple(getattr(d, "coords", None) or ()) or None for d in members]
    ring = Ring(ring_order(coords))
    return jax.shard_map(
        make_local(ring),
        mesh=mesh,
        in_specs=(
            P(("dp", "fsdp"), None),
            P(("dp", "fsdp"), None),
            P(("dp", "fsdp")),
            P(("dp", "fsdp")),
            P(),
            P("fsdp", None),
            P("fsdp", None),
            P("fsdp", None),
            P("fsdp", None),
            P(),
            P("fsdp", None, None),
            P("fsdp", None, None),
            P("fsdp", None, None),
            P("fsdp", None, None),
        ),
        out_specs=(
            P(("dp", "fsdp"), None),
            P(("dp", "fsdp"), None),
            P("fsdp", None),
            P("fsdp", None),
            P("fsdp", None, None),
            P("fsdp", None, None),
            P("fsdp", None),
            P("fsdp", None),
            P("fsdp", None),
            P("fsdp", None),
            P("fsdp", None),
            P(),
            P(),
        ),
        check_vma=False,
    )
```

```python
import jax
import jax.numpy as jnp
from jax import lax
from jax.sharding import PartitionSpec as P

HEAD_DIM = 32
SEQ_LEN = 256
STEP = 5
LANE = 128


EPS_NORM = 1e-05
EPS_ADAM = 1e-08
BETA_FIRST = 0.5
BETA_SECOND = 0.5
RATE_MATRIX = 0.02
RATE_VECTOR = 0.05
EXACT_PRECISION = lax.Precision.HIGHEST
OPT_PRECISION = lax.Precision.HIGH


def normalize_layer(rows_in, norm_gain, norm_shift):
    centred = rows_in - jnp.mean(rows_in, axis=-1, keepdims=True)
    variance = jnp.mean(centred * centred, axis=-1, keepdims=True)
    return centred * lax.rsqrt(variance + EPS_NORM) * norm_gain + norm_shift


def exact_gelu(inputs):
    return jax.nn.gelu(inputs, approximate=False)


def adam_direction(first_new, second_new):
    return (
        first_new
        / (1.0 - BETA_FIRST**STEP)
        / (jnp.sqrt(second_new / (1.0 - BETA_SECOND**STEP)) + EPS_ADAM)
    )


def contract_rows(left_mat, right_mat):
    return jnp.dot(left_mat.T, right_mat, preferred_element_type=jnp.float32)


def times_transpose(left_mat, right_mat):
    return lax.dot_general(
        left_mat, right_mat, (((1,), (1,)), ((), ())), preferred_element_type=jnp.float32
    )


def block_scores(queries, key_rows):
    return jnp.einsum(
        "slhd,smhd->shlm", queries, key_rows, preferred_element_type=jnp.float32
    ) * HEAD_DIM ** (-0.5)


def attend_block(weight_blocks):
    queries, key_rows, values = weight_blocks
    scores = block_scores(queries, key_rows)
    highest = jnp.max(scores, axis=-1, keepdims=True)
    exponent = jnp.exp(scores - highest)
    totals = jnp.sum(exponent, axis=-1, keepdims=True)
    weights_soft = (exponent / totals).astype(jnp.bfloat16)
    mixed_rows = jnp.einsum(
        "shlm,smhd->slhd", weights_soft, values, preferred_element_type=jnp.float32
    )
    return (mixed_rows.astype(jnp.bfloat16), (highest + jnp.log(totals))[..., 0])


def attend_back(weight_blocks):
    queries, key_rows, values, log_total, d_attended = weight_blocks
    probabilities = jnp.exp(block_scores(queries, key_rows) - log_total[..., None])
    d_values = jnp.einsum(
        "shlm,slhd->smhd",
        probabilities.astype(jnp.bfloat16),
        d_attended,
        preferred_element_type=jnp.float32,
    )
    d_probs = jnp.einsum("slhd,smhd->shlm", d_attended, values, preferred_element_type=jnp.float32)
    d_scores = (
        probabilities * (d_probs - jnp.sum(probabilities * d_probs, axis=-1, keepdims=True))
    ).astype(jnp.bfloat16)
    d_queries = jnp.einsum(
        "shlm,smhd->slhd", d_scores, key_rows, preferred_element_type=jnp.float32
    ) * HEAD_DIM ** (-0.5)
    d_keys = jnp.einsum(
        "shlm,slhd->smhd", d_scores, queries, preferred_element_type=jnp.float32
    ) * HEAD_DIM ** (-0.5)
    return (
        d_queries.astype(jnp.bfloat16),
        d_keys.astype(jnp.bfloat16),
        d_values.astype(jnp.bfloat16),
    )


def ring_order(coords):
    count = len(coords)
    if count <= 2 or coords[0] is None:
        return list(range(count))

    def near(a, b):
        return sum(abs(p - q) for p, q in zip(coords[a], coords[b])) == 1

    links = [[b for b in range(count) if near(a, b)] for a in range(count)]
    path, seen, budget = [0], {0}, [20000]

    def extend():
        budget[0] -= 1
        if budget[0] < 0:
            return False
        if len(path) == count:
            return near(path[-1], path[0])
        options = [b for b in links[path[-1]] if b not in seen]
        options.sort(key=lambda b: sum(1 for q in links[b] if q not in seen))
        for b in options:
            path.append(b)
            seen.add(b)
            if extend():
                return True
            path.pop()
            seen.discard(b)
        return False

    return path if extend() else list(range(count))


class Ring:
    def __init__(self, order):
        self.order = order
        self.count = len(order)
        self.forward = [(order[p], order[(p + 1) % self.count]) for p in range(self.count)]
        self.backward = [(order[p], order[(p - 1) % self.count]) for p in range(self.count)]
        position = [0] * self.count
        for p, member in enumerate(order):
            position[member] = p
        self.position = position

    def sources(self):
        me = jnp.asarray(self.position, jnp.int32)[lax.axis_index("fsdp")]
        steps = jnp.arange(self.count, dtype=jnp.int32)
        return jnp.asarray(self.order, jnp.int32)[(me - steps) % self.count]

    def chains(self, width, parts):
        cuts = [round(width * i / (2 * parts) / LANE) * LANE for i in range(2 * parts + 1)]
        cuts[-1] = width
        return [(cuts[i], cuts[i + 1], i % 2 == 0) for i in range(2 * parts)]

    def all_gather(self, local, core, side, core_pairs, parts):
        count = self.count
        mine_cols = lax.dynamic_slice_in_dim(local, core * side, side, axis=1)
        other_cols = lax.dynamic_slice_in_dim(local, (1 - core) * side, side, axis=1)
        mine_parts, other_parts = [], []
        for lo, hi, ahead in self.chains(side, parts):
            pairs = self.forward if ahead else self.backward
            piece = mine_cols[:, lo:hi]
            got, passed = [None] * count, [None] * count
            got[0], passed[0] = piece, other_cols[:, lo:hi]
            for step in range(1, count):
                piece = lax.ppermute(piece, "fsdp", pairs)
                k = step if ahead else count - step
                got[k] = piece
                passed[k] = lax.ppermute(piece, "dp", core_pairs)
            mine_parts.append(got)
            other_parts.append(passed)
        return mine_parts, other_parts

    def reduce_scatter(self, full, rows, outer_pairs, core_pairs, parts):
        count = self.count
        width = full.shape[1]
        outs, partners = [], []
        for lo, hi, ahead in self.chains(width, parts):
            pairs = self.forward if ahead else self.backward

            def block(k):
                return full[k * rows : (k + 1) * rows, lo:hi]

            acc = block(1 % count if ahead else count - 1)
            for step in range(1, count):
                got = lax.ppermute(acc.astype(jnp.bfloat16), "fsdp", pairs)
                k = (step + 1) % count if ahead else (count - step - 1) % count
                acc = got.astype(jnp.float32) + block(k)
            other = lax.ppermute(acc.astype(jnp.bfloat16), "dp", outer_pairs)
            acc = acc + other.astype(jnp.float32)
            outs.append(acc)
            partners.append(lax.ppermute(acc, "dp", core_pairs))
        return jnp.concatenate(outs, axis=1), jnp.concatenate(partners, axis=1)


def make_local(ring):
    def local(
        tokens,
        cotangent,
        masked_pos,
        labels,
        decoder,
        master,
        small_params,
        small_first,
        small_second,
        block_slots,
        first_moment,
        second_moment,
        left_bases,
        right_bases,
    ):
        model_width = decoder.shape[1]
        hidden = (master.shape[1] - 4 * model_width) // 2
        heads_count = model_width // HEAD_DIM
        token_count = tokens.shape[0]
        row_count, weight_cols = master.shape
        small_cols = small_params.shape[1]
        members = lax.axis_size("fsdp")
        core = lax.axis_index("dp") % 2
        replicas = lax.axis_size("dp")
        core_pairs = [(i, i ^ 1) for i in range(replicas)]
        outer_pairs = [(i, i ^ 2) for i in range(replicas)]
        half = weight_cols // 2
        lead = LANE
        side = half + lead
        split = (side // LANE + 1) // 2 * LANE

        sources = ring.sources()
        feature_of = (
            sources[:, None] * row_count + jnp.arange(row_count, dtype=jnp.int32)[None, :]
        ).reshape(-1)
        natural_of = jnp.zeros_like(feature_of).at[feature_of].set(
            jnp.arange(feature_of.shape[0], dtype=jnp.int32)
        )

        picker = (
            jnp.arange(model_width, dtype=jnp.int32)[:, None] == feature_of[None, :]
        ).astype(jnp.bfloat16)

        def to_rel(a):
            return jnp.dot(a, picker, preferred_element_type=jnp.float32).astype(a.dtype)

        def to_nat(a):
            return lax.dot_general(
                a, picker, (((1,), (1,)), ((), ())), precision=EXACT_PRECISION,
                preferred_element_type=jnp.float32,
            )

        w_low = master.astype(jnp.bfloat16)
        s_low = small_params.astype(jnp.bfloat16)
        packed_local = jnp.concatenate(
            [
                s_low,
                jnp.zeros((row_count, lead - small_cols), jnp.bfloat16),
                w_low,
                jnp.zeros((row_count, lead), jnp.bfloat16),
            ],
            axis=1,
        )
        mine, other = ring.all_gather(packed_local, core, side, core_pairs, 1)

        def assemble(first, second):
            return jnp.concatenate(
                [jnp.concatenate(chain, axis=0) for chain in first + second], axis=1
            )

        full = lax.cond(core == 0, lambda: assemble(mine, other), lambda: assemble(other, mine))
        weights = full[:, lead : lead + weight_cols]
        params = jnp.take(full[:, :small_cols].astype(jnp.float32), natural_of, axis=0)

        gain_one, shift_one, bias_query, bias_value, bias_output, gain_two, shift_two, bias_down = [
            params[:, column] for column in range(8)
        ]
        bias_up = params[:, 8:].reshape(hidden)
        rows_in = tokens.astype(jnp.float32)
        normed = normalize_layer(rows_in, gain_one, shift_one).astype(jnp.bfloat16)
        normed_rel = to_rel(normed)
        bias_qkv = jnp.concatenate([bias_query, jnp.zeros_like(bias_query), bias_value])
        projected = (
            jnp.dot(normed_rel, weights[:, : 3 * model_width], preferred_element_type=jnp.float32)
            + bias_qkv
        ).astype(jnp.bfloat16)
        seq_count = token_count // SEQ_LEN
        per_block = max(1, min(seq_count, 512 // SEQ_LEN))
        block_shape = (seq_count // per_block, per_block, SEQ_LEN, heads_count, HEAD_DIM)
        queries = projected[:, :model_width].reshape(block_shape)
        key_rows = projected[:, model_width : 2 * model_width].reshape(block_shape)
        values = projected[:, 2 * model_width :].reshape(block_shape)
        attention_result, log_total = lax.map(attend_block, (queries, key_rows, values))
        attention_result = attention_result.reshape(token_count, model_width)
        attended_rel = to_rel(attention_result)
        middle = (
            rows_in
            + jnp.dot(
                attended_rel,
                weights[:, 3 * model_width : 4 * model_width],
                preferred_element_type=jnp.float32,
            )
            + bias_output
        )
        normed_two = normalize_layer(middle, gain_two, shift_two).astype(jnp.bfloat16)
        normed_two_rel = to_rel(normed_two)
        pre_active = (
            jnp.dot(
                normed_two_rel,
                weights[:, 4 * model_width : 4 * model_width + hidden],
                preferred_element_type=jnp.float32,
            )
            + bias_up
        )
        active = exact_gelu(pre_active).astype(jnp.bfloat16)
        output_rows = (
            middle
            + to_nat(times_transpose(active, weights[:, 4 * model_width + hidden :]))
            + bias_down
        )
        out_tokens = output_rows.astype(jnp.bfloat16)
        logits = times_transpose(out_tokens, decoder)
        log_norm = jax.nn.logsumexp(logits, axis=-1)
        one_hot = (
            labels[:, None] == jnp.arange(decoder.shape[0], dtype=jnp.int32)[None, :]
        ).astype(jnp.float32)
        hidden_tokens = masked_pos.astype(jnp.float32)
        chosen = one_hot * hidden_tokens[:, None]
        entropy = log_norm - jnp.sum(one_hot * logits, axis=-1)
        right_prob = jnp.sum(one_hot * jnp.exp(logits - log_norm[:, None]), axis=-1)
        local_sums = jnp.concatenate(
            [jnp.sum(hidden_tokens * entropy)[None], jnp.sum(chosen * right_prob[:, None], axis=0)]
        )
        totals = jnp.concatenate([local_sums, jnp.sum(chosen, axis=0)])
        for axis in ("dp", "fsdp"):
            size = lax.axis_size(axis)
            reach = 1
            while reach < size:
                totals = totals + lax.ppermute(
                    totals, axis, [(i, i ^ reach) for i in range(size)]
                )
                reach *= 2
        global_sums, global_counts = totals[: local_sums.shape[0]], totals[local_sums.shape[0] :]
        loss_accuracy = jnp.concatenate(
            [
                global_sums[:1] / jnp.maximum(jnp.sum(global_counts), 1.0),
                global_sums[1:] / jnp.maximum(global_counts, 1.0),
            ]
        )
        counts = global_counts.astype(jnp.int32)
        back_rows = cotangent.astype(jnp.float32)
        cotangent_rel = to_rel(cotangent)
        d_active = jnp.dot(
            cotangent_rel, weights[:, 4 * model_width + hidden :], preferred_element_type=jnp.float32
        )
        unused, gelu_pull = jax.vjp(exact_gelu, pre_active)
        d_pre = gelu_pull(d_active)[0].astype(jnp.bfloat16)
        d_normed_two = to_nat(
            times_transpose(d_pre, weights[:, 4 * model_width : 4 * model_width + hidden])
        )
        unused, norm_pull_two = jax.vjp(normalize_layer, middle, params[:, 5], params[:, 6])
        d_middle_norm, d_gain_two, d_shift_two = norm_pull_two(d_normed_two)
        d_middle = back_rows + d_middle_norm
        d_branch = d_middle.astype(jnp.bfloat16)
        d_attended = to_nat(
            times_transpose(d_branch, weights[:, 3 * model_width : 4 * model_width])
        ).astype(jnp.bfloat16)
        d_queries, d_keys, d_values = lax.map(
            attend_back, (queries, key_rows, values, log_total, d_attended.reshape(block_shape))
        )
        d_projected = jnp.concatenate(
            [
                d_queries.reshape(token_count, model_width),
                d_keys.reshape(token_count, model_width),
                d_values.reshape(token_count, model_width),
            ],
            axis=1,
        )
        d_normed = to_nat(times_transpose(d_projected, weights[:, : 3 * model_width]))
        unused, norm_pull_one = jax.vjp(normalize_layer, rows_in, params[:, 0], params[:, 1])
        d_rows_norm, d_gain_one, d_shift_one = norm_pull_one(d_normed)
        grad_tokens = (d_middle + d_rows_norm).astype(jnp.bfloat16)
        proj_sums = jnp.sum(d_projected.astype(jnp.float32), axis=0)
        small_grads = jnp.stack(
            [
                d_gain_one,
                d_shift_one,
                proj_sums[:model_width],
                proj_sums[2 * model_width :],
                jnp.sum(d_branch.astype(jnp.float32), axis=0),
                d_gain_two,
                d_shift_two,
                jnp.sum(back_rows, axis=0),
            ],
            axis=1,
        )
        small_grads = jnp.concatenate(
            [small_grads, jnp.sum(d_pre.astype(jnp.float32), axis=0).reshape(model_width, -1)], axis=1
        )
        small_rel = jnp.take(small_grads, feature_of, axis=0)
        up_first = side - lead - 4 * model_width

        def halves(flip):
            def build():
                grad_up = contract_rows(normed_two_rel, d_pre)
                first = jnp.concatenate(
                    [
                        small_rel,
                        jnp.zeros((model_width, lead - small_cols), jnp.float32),
                        contract_rows(normed_rel, d_projected),
                        contract_rows(attended_rel, d_branch),
                        grad_up[:, :up_first],
                    ],
                    axis=1,
                )
                second = jnp.concatenate(
                    [
                        grad_up[:, up_first:],
                        contract_rows(cotangent_rel, active),
                        jnp.zeros((model_width, lead), jnp.float32),
                    ],
                    axis=1,
                )
                kept, given = (second, first) if flip else (first, second)
                return kept, given.astype(jnp.bfloat16)

            return build

        keep, send = lax.cond(core == 0, halves(False), halves(True))
        chip = keep + lax.ppermute(send, "dp", core_pairs).astype(jnp.float32)
        total, partner = ring.reduce_scatter(chip, row_count, outer_pairs, core_pairs, 2)
        joined = lax.cond(
            core == 0,
            lambda a, b: jnp.concatenate([a, b], axis=1),
            lambda a, b: jnp.concatenate([b, a], axis=1),
            total,
            partner,
        )
        grad_w = joined[:, lead : lead + weight_cols]
        grad_s = joined[:, :small_cols]

        block_width = model_width // 2
        block_count = grad_w.shape[1] // block_width
        owned_slots = first_moment.shape[0]
        devices = members
        slot_ids = jnp.arange(owned_slots * devices, dtype=jnp.int32)
        matches = block_slots[None, :] == slot_ids[:, None]
        in_use = jnp.any(matches, axis=1)
        source_block = jnp.sum(
            jnp.where(matches, jnp.arange(block_count, dtype=jnp.int32)[None, :], 0), axis=1
        )
        quarter = block_width // 2
        outgoing = jnp.take(grad_w.reshape(row_count, block_count, block_width), source_block, axis=1)
        outgoing = lax.dynamic_slice_in_dim(outgoing, core * quarter, quarter, axis=2)
        outgoing = jnp.where(in_use[None, :, None], outgoing, 0.0).reshape(
            row_count, devices, owned_slots, quarter
        )
        incoming = lax.all_to_all(
            outgoing.astype(jnp.bfloat16), "fsdp", split_axis=1, concat_axis=0, tiled=True
        ).reshape(row_count * devices, owned_slots, quarter)
        incoming_other = lax.ppermute(incoming, "dp", core_pairs)
        incoming = lax.cond(
            core == 0,
            lambda: jnp.concatenate([incoming, incoming_other], axis=2),
            lambda: jnp.concatenate([incoming_other, incoming], axis=2),
        ).astype(jnp.float32)
        my_use = lax.dynamic_slice_in_dim(in_use, lax.axis_index("fsdp") * owned_slots, owned_slots)
        eigen_turned = jnp.einsum("kdi,dkc->kic", left_bases, incoming, precision=OPT_PRECISION)
        eigen_turned = jnp.einsum("kic,kcj->kij", eigen_turned, right_bases, precision=OPT_PRECISION)
        first_new = BETA_FIRST * first_moment + (1.0 - BETA_FIRST) * eigen_turned
        second_new = BETA_SECOND * second_moment + (1.0 - BETA_SECOND) * eigen_turned * eigen_turned
        direction = adam_direction(first_new, second_new)
        rotated_gradient = jnp.einsum("kij,klj->kil", direction, right_bases, precision=OPT_PRECISION)
        rotated_gradient = jnp.einsum(
            "kdi,kil->dkl", left_bases, rotated_gradient, precision=OPT_PRECISION
        )
        going = lax.dynamic_slice_in_dim(rotated_gradient, core * quarter, quarter, axis=2)
        returned = lax.all_to_all(
            going.reshape(devices, row_count, owned_slots, quarter).astype(jnp.bfloat16),
            "fsdp",
            split_axis=0,
            concat_axis=0,
            tiled=True,
        )
        returned_other = lax.ppermute(returned, "dp", core_pairs)
        returned_full = lax.cond(
            core == 0,
            lambda: jnp.concatenate([returned, returned_other], axis=3),
            lambda: jnp.concatenate([returned_other, returned], axis=3),
        )
        owner_of = block_slots // owned_slots
        slot_in = block_slots % owned_slots
        update = returned_full[owner_of, :, slot_in, :].astype(jnp.float32)
        update = jnp.transpose(update, (1, 0, 2)).reshape(row_count, block_count * block_width)
        new_master = master - RATE_MATRIX * update
        new_copy = new_master.astype(jnp.bfloat16)
        keep_slot = my_use[:, None, None]
        new_first = jnp.where(keep_slot, first_new, 0.0)
        new_second = jnp.where(keep_slot, second_new, 0.0)
        new_small_first = BETA_FIRST * small_first + (1.0 - BETA_FIRST) * grad_s
        new_small_second = BETA_SECOND * small_second + (1.0 - BETA_SECOND) * grad_s * grad_s
        new_small = small_params - RATE_VECTOR * adam_direction(new_small_first, new_small_second)
        return (
            out_tokens,
            grad_tokens,
            grad_w,
            grad_s,
            new_first,
            new_second,
            new_master,
            new_copy,
            new_small,
            new_small_first,
            new_small_second,
            loss_accuracy,
            counts,
        )

    return local


def solution(mesh):
    members = mesh.devices[0]
    coords = [tuple(getattr(d, "coords", None) or ()) or None for d in members]
    ring = Ring(ring_order(coords))
    return jax.shard_map(
        make_local(ring),
        mesh=mesh,
        in_specs=(
            P(("dp", "fsdp"), None),
            P(("dp", "fsdp"), None),
            P(("dp", "fsdp")),
            P(("dp", "fsdp")),
            P(),
            P("fsdp", None),
            P("fsdp", None),
            P("fsdp", None),
            P("fsdp", None),
            P(),
            P("fsdp", None, None),
            P("fsdp", None, None),
            P("fsdp", None, None),
            P("fsdp", None, None),
        ),
        out_specs=(
            P(("dp", "fsdp"), None),
            P(("dp", "fsdp"), None),
            P("fsdp", None),
            P("fsdp", None),
            P("fsdp", None, None),
            P("fsdp", None, None),
            P("fsdp", None),
            P("fsdp", None),
            P("fsdp", None),
            P("fsdp", None),
            P("fsdp", None),
            P(),
            P(),
        ),
        check_vma=False,
    )
```

```python
import jax
import jax.numpy as jnp
from jax import lax
from jax.sharding import PartitionSpec as P

HEAD_DIM = 32
SEQ_LEN = 256
STEP = 5
LANE = 128


EPS_NORM = 1e-05
EPS_ADAM = 1e-08
BETA_FIRST = 0.5
BETA_SECOND = 0.5
RATE_MATRIX = 0.02
RATE_VECTOR = 0.05
EXACT_PRECISION = lax.Precision.HIGHEST
OPT_PRECISION = lax.Precision.HIGH


def normalize_layer(rows_in, norm_gain, norm_shift):
    centred = rows_in - jnp.mean(rows_in, axis=-1, keepdims=True)
    variance = jnp.mean(centred * centred, axis=-1, keepdims=True)
    return centred * lax.rsqrt(variance + EPS_NORM) * norm_gain + norm_shift


def exact_gelu(inputs):
    return jax.nn.gelu(inputs, approximate=False)


def adam_direction(first_new, second_new):
    return (
        first_new
        / (1.0 - BETA_FIRST**STEP)
        / (jnp.sqrt(second_new / (1.0 - BETA_SECOND**STEP)) + EPS_ADAM)
    )


def contract_rows(left_mat, right_mat):
    return jnp.dot(left_mat.T, right_mat, preferred_element_type=jnp.float32)


def times_transpose(left_mat, right_mat):
    return lax.dot_general(
        left_mat, right_mat, (((1,), (1,)), ((), ())), preferred_element_type=jnp.float32
    )


def block_scores(queries, key_rows):
    return jnp.einsum(
        "slhd,smhd->shlm", queries, key_rows, preferred_element_type=jnp.float32
    ) * HEAD_DIM ** (-0.5)


def attend_block(weight_blocks):
    queries, key_rows, values = weight_blocks
    scores = block_scores(queries, key_rows)
    highest = jnp.max(scores, axis=-1, keepdims=True)
    exponent = jnp.exp(scores - highest)
    totals = jnp.sum(exponent, axis=-1, keepdims=True)
    weights_soft = (exponent / totals).astype(jnp.bfloat16)
    mixed_rows = jnp.einsum(
        "shlm,smhd->slhd", weights_soft, values, preferred_element_type=jnp.float32
    )
    return (mixed_rows.astype(jnp.bfloat16), (highest + jnp.log(totals))[..., 0])


def attend_back(weight_blocks):
    queries, key_rows, values, log_total, d_attended = weight_blocks
    probabilities = jnp.exp(block_scores(queries, key_rows) - log_total[..., None])
    d_values = jnp.einsum(
        "shlm,slhd->smhd",
        probabilities.astype(jnp.bfloat16),
        d_attended,
        preferred_element_type=jnp.float32,
    )
    d_probs = jnp.einsum("slhd,smhd->shlm", d_attended, values, preferred_element_type=jnp.float32)
    d_scores = (
        probabilities * (d_probs - jnp.sum(probabilities * d_probs, axis=-1, keepdims=True))
    ).astype(jnp.bfloat16)
    d_queries = jnp.einsum(
        "shlm,smhd->slhd", d_scores, key_rows, preferred_element_type=jnp.float32
    ) * HEAD_DIM ** (-0.5)
    d_keys = jnp.einsum(
        "shlm,slhd->smhd", d_scores, queries, preferred_element_type=jnp.float32
    ) * HEAD_DIM ** (-0.5)
    return (
        d_queries.astype(jnp.bfloat16),
        d_keys.astype(jnp.bfloat16),
        d_values.astype(jnp.bfloat16),
    )


def ring_order(coords):
    count = len(coords)
    if count <= 2 or coords[0] is None:
        return list(range(count))

    def near(a, b):
        return sum(abs(p - q) for p, q in zip(coords[a], coords[b])) == 1

    links = [[b for b in range(count) if near(a, b)] for a in range(count)]
    path, seen, budget = [0], {0}, [20000]

    def extend():
        budget[0] -= 1
        if budget[0] < 0:
            return False
        if len(path) == count:
            return near(path[-1], path[0])
        options = [b for b in links[path[-1]] if b not in seen]
        options.sort(key=lambda b: sum(1 for q in links[b] if q not in seen))
        for b in options:
            path.append(b)
            seen.add(b)
            if extend():
                return True
            path.pop()
            seen.discard(b)
        return False

    return path if extend() else list(range(count))


class Ring:
    def __init__(self, order):
        self.order = order
        self.count = len(order)
        self.forward = [(order[p], order[(p + 1) % self.count]) for p in range(self.count)]
        self.backward = [(order[p], order[(p - 1) % self.count]) for p in range(self.count)]
        position = [0] * self.count
        for p, member in enumerate(order):
            position[member] = p
        self.position = position

    def sources(self):
        me = jnp.asarray(self.position, jnp.int32)[lax.axis_index("fsdp")]
        steps = jnp.arange(self.count, dtype=jnp.int32)
        return jnp.asarray(self.order, jnp.int32)[(me - steps) % self.count]

    def chains(self, width, parts):
        cuts = [round(width * i / (2 * parts) / LANE) * LANE for i in range(2 * parts + 1)]
        cuts[-1] = width
        return [(cuts[i], cuts[i + 1], i % 2 == 0) for i in range(2 * parts)]

    def all_gather(self, local, core, side, core_pairs, parts):
        count = self.count
        mine_cols = lax.dynamic_slice_in_dim(local, core * side, side, axis=1)
        other_cols = lax.dynamic_slice_in_dim(local, (1 - core) * side, side, axis=1)
        mine_parts, other_parts = [], []
        for lo, hi, ahead in self.chains(side, parts):
            pairs = self.forward if ahead else self.backward
            piece = mine_cols[:, lo:hi]
            got, passed = [None] * count, [None] * count
            got[0], passed[0] = piece, other_cols[:, lo:hi]
            for step in range(1, count):
                piece = lax.ppermute(piece, "fsdp", pairs)
                k = step if ahead else count - step
                got[k] = piece
                passed[k] = lax.ppermute(piece, "dp", core_pairs)
            mine_parts.append(got)
            other_parts.append(passed)
        return mine_parts, other_parts

    def reduce_scatter(self, full, rows, outer_pairs, core_pairs, parts):
        count = self.count
        width = full.shape[1]
        outs, partners = [], []
        for lo, hi, ahead in self.chains(width, parts):
            pairs = self.forward if ahead else self.backward

            def block(k):
                return full[k * rows : (k + 1) * rows, lo:hi]

            acc = block(1 % count if ahead else count - 1)
            for step in range(1, count):
                got = lax.ppermute(acc.astype(jnp.bfloat16), "fsdp", pairs)
                k = (step + 1) % count if ahead else (count - step - 1) % count
                acc = got.astype(jnp.float32) + block(k)
            other = lax.ppermute(acc.astype(jnp.bfloat16), "dp", outer_pairs)
            acc = acc + other.astype(jnp.float32)
            outs.append(acc)
            partners.append(lax.ppermute(acc, "dp", core_pairs))
        return jnp.concatenate(outs, axis=1), jnp.concatenate(partners, axis=1)


def make_local(ring):
    def local(
        tokens,
        cotangent,
        masked_pos,
        labels,
        decoder,
        master,
        small_params,
        small_first,
        small_second,
        block_slots,
        first_moment,
        second_moment,
        left_bases,
        right_bases,
    ):
        model_width = decoder.shape[1]
        hidden = (master.shape[1] - 4 * model_width) // 2
        heads_count = model_width // HEAD_DIM
        token_count = tokens.shape[0]
        row_count, weight_cols = master.shape
        small_cols = small_params.shape[1]
        members = lax.axis_size("fsdp")
        core = lax.axis_index("dp") % 2
        replicas = lax.axis_size("dp")
        core_pairs = [(i, i ^ 1) for i in range(replicas)]
        outer_pairs = [(i, i ^ 2) for i in range(replicas)]
        half = weight_cols // 2
        lead = LANE
        side = half + lead
        split = (side // LANE + 1) // 2 * LANE

        sources = ring.sources()
        feature_of = (
            sources[:, None] * row_count + jnp.arange(row_count, dtype=jnp.int32)[None, :]
        ).reshape(-1)
        natural_of = jnp.zeros_like(feature_of).at[feature_of].set(
            jnp.arange(feature_of.shape[0], dtype=jnp.int32)
        )

        picker = (
            jnp.arange(model_width, dtype=jnp.int32)[:, None] == feature_of[None, :]
        ).astype(jnp.bfloat16)

        def to_rel(a):
            return jnp.dot(a, picker, preferred_element_type=jnp.float32).astype(a.dtype)

        def to_nat(a):
            return lax.dot_general(
                a, picker, (((1,), (1,)), ((), ())), precision=EXACT_PRECISION,
                preferred_element_type=jnp.float32,
            )

        w_low = master.astype(jnp.bfloat16)
        s_low = small_params.astype(jnp.bfloat16)
        packed_local = jnp.concatenate(
            [
                s_low,
                jnp.zeros((row_count, lead - small_cols), jnp.bfloat16),
                w_low,
                jnp.zeros((row_count, lead), jnp.bfloat16),
            ],
            axis=1,
        )
        mine, other = ring.all_gather(packed_local, core, side, core_pairs, 1)

        def assemble(first, second):
            return jnp.concatenate(
                [jnp.concatenate(chain, axis=0) for chain in first + second], axis=1
            )

        full = lax.cond(core == 0, lambda: assemble(mine, other), lambda: assemble(other, mine))
        weights = full[:, lead : lead + weight_cols]
        params = jnp.take(full[:, :small_cols].astype(jnp.float32), natural_of, axis=0)

        gain_one, shift_one, bias_query, bias_value, bias_output, gain_two, shift_two, bias_down = [
            params[:, column] for column in range(8)
        ]
        bias_up = params[:, 8:].reshape(hidden)
        rows_in = tokens.astype(jnp.float32)
        normed = normalize_layer(rows_in, gain_one, shift_one).astype(jnp.bfloat16)
        normed_rel = to_rel(normed)
        bias_qkv = jnp.concatenate([bias_query, jnp.zeros_like(bias_query), bias_value])
        projected = (
            jnp.dot(normed_rel, weights[:, : 3 * model_width], preferred_element_type=jnp.float32)
            + bias_qkv
        ).astype(jnp.bfloat16)
        seq_count = token_count // SEQ_LEN
        per_block = max(1, min(seq_count, 512 // SEQ_LEN))
        block_shape = (seq_count // per_block, per_block, SEQ_LEN, heads_count, HEAD_DIM)
        queries = projected[:, :model_width].reshape(block_shape)
        key_rows = projected[:, model_width : 2 * model_width].reshape(block_shape)
        values = projected[:, 2 * model_width :].reshape(block_shape)
        attention_result, log_total = lax.map(attend_block, (queries, key_rows, values))
        attention_result = attention_result.reshape(token_count, model_width)
        attended_rel = to_rel(attention_result)
        middle = (
            rows_in
            + jnp.dot(
                attended_rel,
                weights[:, 3 * model_width : 4 * model_width],
                preferred_element_type=jnp.float32,
            )
            + bias_output
        )
        normed_two = normalize_layer(middle, gain_two, shift_two).astype(jnp.bfloat16)
        normed_two_rel = to_rel(normed_two)
        pre_active = (
            jnp.dot(
                normed_two_rel,
                weights[:, 4 * model_width : 4 * model_width + hidden],
                preferred_element_type=jnp.float32,
            )
            + bias_up
        )
        active = exact_gelu(pre_active).astype(jnp.bfloat16)
        output_rows = (
            middle
            + to_nat(times_transpose(active, weights[:, 4 * model_width + hidden :]))
            + bias_down
        )
        out_tokens = output_rows.astype(jnp.bfloat16)
        logits = times_transpose(out_tokens, decoder)
        log_norm = jax.nn.logsumexp(logits, axis=-1)
        one_hot = (
            labels[:, None] == jnp.arange(decoder.shape[0], dtype=jnp.int32)[None, :]
        ).astype(jnp.float32)
        hidden_tokens = masked_pos.astype(jnp.float32)
        chosen = one_hot * hidden_tokens[:, None]
        entropy = log_norm - jnp.sum(one_hot * logits, axis=-1)
        right_prob = jnp.sum(one_hot * jnp.exp(logits - log_norm[:, None]), axis=-1)
        local_sums = jnp.concatenate(
            [jnp.sum(hidden_tokens * entropy)[None], jnp.sum(chosen * right_prob[:, None], axis=0)]
        )
        totals = jnp.concatenate([local_sums, jnp.sum(chosen, axis=0)])
        for axis in ("dp", "fsdp"):
            size = lax.axis_size(axis)
            reach = 1
            while reach < size:
                totals = totals + lax.ppermute(
                    totals, axis, [(i, i ^ reach) for i in range(size)]
                )
                reach *= 2
        global_sums, global_counts = totals[: local_sums.shape[0]], totals[local_sums.shape[0] :]
        loss_accuracy = jnp.concatenate(
            [
                global_sums[:1] / jnp.maximum(jnp.sum(global_counts), 1.0),
                global_sums[1:] / jnp.maximum(global_counts, 1.0),
            ]
        )
        counts = global_counts.astype(jnp.int32)
        back_rows = cotangent.astype(jnp.float32)
        cotangent_rel = to_rel(cotangent)
        d_active = jnp.dot(
            cotangent_rel, weights[:, 4 * model_width + hidden :], preferred_element_type=jnp.float32
        )
        unused, gelu_pull = jax.vjp(exact_gelu, pre_active)
        d_pre = gelu_pull(d_active)[0].astype(jnp.bfloat16)
        d_normed_two = to_nat(
            times_transpose(d_pre, weights[:, 4 * model_width : 4 * model_width + hidden])
        )
        unused, norm_pull_two = jax.vjp(normalize_layer, middle, params[:, 5], params[:, 6])
        d_middle_norm, d_gain_two, d_shift_two = norm_pull_two(d_normed_two)
        d_middle = back_rows + d_middle_norm
        d_branch = d_middle.astype(jnp.bfloat16)
        d_attended = to_nat(
            times_transpose(d_branch, weights[:, 3 * model_width : 4 * model_width])
        ).astype(jnp.bfloat16)
        d_queries, d_keys, d_values = lax.map(
            attend_back, (queries, key_rows, values, log_total, d_attended.reshape(block_shape))
        )
        d_projected = jnp.concatenate(
            [
                d_queries.reshape(token_count, model_width),
                d_keys.reshape(token_count, model_width),
                d_values.reshape(token_count, model_width),
            ],
            axis=1,
        )
        d_normed = to_nat(times_transpose(d_projected, weights[:, : 3 * model_width]))
        unused, norm_pull_one = jax.vjp(normalize_layer, rows_in, params[:, 0], params[:, 1])
        d_rows_norm, d_gain_one, d_shift_one = norm_pull_one(d_normed)
        grad_tokens = (d_middle + d_rows_norm).astype(jnp.bfloat16)
        proj_sums = jnp.sum(d_projected.astype(jnp.float32), axis=0)
        small_grads = jnp.stack(
            [
                d_gain_one,
                d_shift_one,
                proj_sums[:model_width],
                proj_sums[2 * model_width :],
                jnp.sum(d_branch.astype(jnp.float32), axis=0),
                d_gain_two,
                d_shift_two,
                jnp.sum(back_rows, axis=0),
            ],
            axis=1,
        )
        small_grads = jnp.concatenate(
            [small_grads, jnp.sum(d_pre.astype(jnp.float32), axis=0).reshape(model_width, -1)], axis=1
        )
        small_rel = jnp.take(small_grads, feature_of, axis=0)
        up_first = side - lead - 4 * model_width

        def halves(flip):
            def build():
                grad_up = contract_rows(normed_two_rel, d_pre)
                first = jnp.concatenate(
                    [
                        small_rel,
                        jnp.zeros((model_width, lead - small_cols), jnp.float32),
                        contract_rows(normed_rel, d_projected),
                        contract_rows(attended_rel, d_branch),
                        grad_up[:, :up_first],
                    ],
                    axis=1,
                )
                second = jnp.concatenate(
                    [
                        grad_up[:, up_first:],
                        contract_rows(cotangent_rel, active),
                        jnp.zeros((model_width, lead), jnp.float32),
                    ],
                    axis=1,
                )
                kept, given = (second, first) if flip else (first, second)
                return kept, given.astype(jnp.bfloat16)

            return build

        keep, send = lax.cond(core == 0, halves(False), halves(True))
        chip = keep + lax.ppermute(send, "dp", core_pairs).astype(jnp.float32)
        total, partner = ring.reduce_scatter(chip, row_count, outer_pairs, core_pairs, 2)
        joined = lax.cond(
            core == 0,
            lambda a, b: jnp.concatenate([a, b], axis=1),
            lambda a, b: jnp.concatenate([b, a], axis=1),
            total,
            partner,
        )
        grad_w = joined[:, lead : lead + weight_cols]
        grad_s = joined[:, :small_cols]

        block_width = model_width // 2
        block_count = grad_w.shape[1] // block_width
        owned_slots = first_moment.shape[0]
        devices = members
        slot_ids = jnp.arange(owned_slots * devices, dtype=jnp.int32)
        matches = block_slots[None, :] == slot_ids[:, None]
        in_use = jnp.any(matches, axis=1)
        source_block = jnp.sum(
            jnp.where(matches, jnp.arange(block_count, dtype=jnp.int32)[None, :], 0), axis=1
        )
        quarter = block_width // 2
        outgoing = jnp.take(grad_w.reshape(row_count, block_count, block_width), source_block, axis=1)
        outgoing = lax.dynamic_slice_in_dim(outgoing, core * quarter, quarter, axis=2)
        outgoing = jnp.where(in_use[None, :, None], outgoing, 0.0).reshape(
            row_count, devices, owned_slots, quarter
        )
        outgoing = jnp.transpose(outgoing, (2, 0, 1, 3)).astype(jnp.bfloat16)
        incoming = lax.all_to_all(
            outgoing, "fsdp", split_axis=2, concat_axis=1, tiled=True
        ).reshape(owned_slots, row_count * devices, quarter)
        incoming_other = lax.ppermute(incoming, "dp", core_pairs)
        incoming = lax.cond(
            core == 0,
            lambda: jnp.concatenate([incoming, incoming_other], axis=2),
            lambda: jnp.concatenate([incoming_other, incoming], axis=2),
        ).astype(jnp.float32)
        my_use = lax.dynamic_slice_in_dim(in_use, lax.axis_index("fsdp") * owned_slots, owned_slots)
        eigen_turned = jnp.einsum("kdi,kdc->kic", left_bases, incoming, precision=OPT_PRECISION)
        eigen_turned = jnp.einsum("kic,kcj->kij", eigen_turned, right_bases, precision=OPT_PRECISION)
        first_new = BETA_FIRST * first_moment + (1.0 - BETA_FIRST) * eigen_turned
        second_new = BETA_SECOND * second_moment + (1.0 - BETA_SECOND) * eigen_turned * eigen_turned
        direction = adam_direction(first_new, second_new)
        rotated_gradient = jnp.einsum("kij,klj->kil", direction, right_bases, precision=OPT_PRECISION)
        rotated_gradient = jnp.einsum(
            "kdi,kil->kdl", left_bases, rotated_gradient, precision=OPT_PRECISION
        )
        going = lax.dynamic_slice_in_dim(rotated_gradient, core * quarter, quarter, axis=2)
        returned = lax.all_to_all(
            going.reshape(owned_slots, devices, row_count, quarter).astype(jnp.bfloat16),
            "fsdp",
            split_axis=1,
            concat_axis=1,
            tiled=True,
        )
        returned_other = lax.ppermute(returned, "dp", core_pairs)
        returned_full = lax.cond(
            core == 0,
            lambda: jnp.concatenate([returned, returned_other], axis=3),
            lambda: jnp.concatenate([returned_other, returned], axis=3),
        ).reshape(owned_slots * devices, row_count, block_width)
        slot_row = (block_slots % owned_slots) * devices + block_slots // owned_slots
        update = jnp.take(returned_full, slot_row, axis=0).astype(jnp.float32)
        update = jnp.transpose(update, (1, 0, 2)).reshape(row_count, block_count * block_width)
        new_master = master - RATE_MATRIX * update
        new_copy = new_master.astype(jnp.bfloat16)
        keep_slot = my_use[:, None, None]
        new_first = jnp.where(keep_slot, first_new, 0.0)
        new_second = jnp.where(keep_slot, second_new, 0.0)
        new_small_first = BETA_FIRST * small_first + (1.0 - BETA_FIRST) * grad_s
        new_small_second = BETA_SECOND * small_second + (1.0 - BETA_SECOND) * grad_s * grad_s
        new_small = small_params - RATE_VECTOR * adam_direction(new_small_first, new_small_second)
        return (
            out_tokens,
            grad_tokens,
            grad_w,
            grad_s,
            new_first,
            new_second,
            new_master,
            new_copy,
            new_small,
            new_small_first,
            new_small_second,
            loss_accuracy,
            counts,
        )

    return local


def solution(mesh):
    members = mesh.devices[0]
    coords = [tuple(getattr(d, "coords", None) or ()) or None for d in members]
    ring = Ring(ring_order(coords))
    return jax.shard_map(
        make_local(ring),
        mesh=mesh,
        in_specs=(
            P(("dp", "fsdp"), None),
            P(("dp", "fsdp"), None),
            P(("dp", "fsdp")),
            P(("dp", "fsdp")),
            P(),
            P("fsdp", None),
            P("fsdp", None),
            P("fsdp", None),
            P("fsdp", None),
            P(),
            P("fsdp", None, None),
            P("fsdp", None, None),
            P("fsdp", None, None),
            P("fsdp", None, None),
        ),
        out_specs=(
            P(("dp", "fsdp"), None),
            P(("dp", "fsdp"), None),
            P("fsdp", None),
            P("fsdp", None),
            P("fsdp", None, None),
            P("fsdp", None, None),
            P("fsdp", None),
            P("fsdp", None),
            P("fsdp", None),
            P("fsdp", None),
            P("fsdp", None),
            P(),
            P(),
        ),
        check_vma=False,
    )
```

```python
import jax
import jax.numpy as jnp
from jax import lax
from jax.sharding import PartitionSpec as P

HEAD_DIM = 32
SEQ_LEN = 256
STEP = 5
LANE = 128


EPS_NORM = 1e-05
EPS_ADAM = 1e-08
BETA_FIRST = 0.5
BETA_SECOND = 0.5
RATE_MATRIX = 0.02
RATE_VECTOR = 0.05
EXACT_PRECISION = lax.Precision.HIGHEST
OPT_PRECISION = lax.Precision.HIGH


def normalize_layer(rows_in, norm_gain, norm_shift):
    centred = rows_in - jnp.mean(rows_in, axis=-1, keepdims=True)
    variance = jnp.mean(centred * centred, axis=-1, keepdims=True)
    return centred * lax.rsqrt(variance + EPS_NORM) * norm_gain + norm_shift


def exact_gelu(inputs):
    return jax.nn.gelu(inputs, approximate=False)


def adam_direction(first_new, second_new):
    return (
        first_new
        / (1.0 - BETA_FIRST**STEP)
        / (jnp.sqrt(second_new / (1.0 - BETA_SECOND**STEP)) + EPS_ADAM)
    )


def contract_rows(left_mat, right_mat):
    return jnp.dot(left_mat.T, right_mat, preferred_element_type=jnp.float32)


def times_transpose(left_mat, right_mat):
    return lax.dot_general(
        left_mat, right_mat, (((1,), (1,)), ((), ())), preferred_element_type=jnp.float32
    )


def block_scores(queries, key_rows):
    return jnp.einsum(
        "slhd,smhd->shlm", queries, key_rows, preferred_element_type=jnp.float32
    ) * HEAD_DIM ** (-0.5)


def attend_block(weight_blocks):
    queries, key_rows, values = weight_blocks
    scores = block_scores(queries, key_rows)
    highest = jnp.max(scores, axis=-1, keepdims=True)
    exponent = jnp.exp(scores - highest)
    totals = jnp.sum(exponent, axis=-1, keepdims=True)
    weights_soft = (exponent / totals).astype(jnp.bfloat16)
    mixed_rows = jnp.einsum(
        "shlm,smhd->slhd", weights_soft, values, preferred_element_type=jnp.float32
    )
    return (mixed_rows.astype(jnp.bfloat16), (highest + jnp.log(totals))[..., 0])


def attend_back(weight_blocks):
    queries, key_rows, values, log_total, d_attended = weight_blocks
    probabilities = jnp.exp(block_scores(queries, key_rows) - log_total[..., None])
    d_values = jnp.einsum(
        "shlm,slhd->smhd",
        probabilities.astype(jnp.bfloat16),
        d_attended,
        preferred_element_type=jnp.float32,
    )
    d_probs = jnp.einsum("slhd,smhd->shlm", d_attended, values, preferred_element_type=jnp.float32)
    d_scores = (
        probabilities * (d_probs - jnp.sum(probabilities * d_probs, axis=-1, keepdims=True))
    ).astype(jnp.bfloat16)
    d_queries = jnp.einsum(
        "shlm,smhd->slhd", d_scores, key_rows, preferred_element_type=jnp.float32
    ) * HEAD_DIM ** (-0.5)
    d_keys = jnp.einsum(
        "shlm,slhd->smhd", d_scores, queries, preferred_element_type=jnp.float32
    ) * HEAD_DIM ** (-0.5)
    return (
        d_queries.astype(jnp.bfloat16),
        d_keys.astype(jnp.bfloat16),
        d_values.astype(jnp.bfloat16),
    )


def ring_order(coords):
    count = len(coords)
    if count <= 2 or coords[0] is None:
        return list(range(count))

    def near(a, b):
        return sum(abs(p - q) for p, q in zip(coords[a], coords[b])) == 1

    links = [[b for b in range(count) if near(a, b)] for a in range(count)]
    path, seen, budget = [0], {0}, [20000]

    def extend():
        budget[0] -= 1
        if budget[0] < 0:
            return False
        if len(path) == count:
            return near(path[-1], path[0])
        options = [b for b in links[path[-1]] if b not in seen]
        options.sort(key=lambda b: sum(1 for q in links[b] if q not in seen))
        for b in options:
            path.append(b)
            seen.add(b)
            if extend():
                return True
            path.pop()
            seen.discard(b)
        return False

    return path if extend() else list(range(count))


class Ring:
    def __init__(self, order):
        self.order = order
        self.count = len(order)
        self.forward = [(order[p], order[(p + 1) % self.count]) for p in range(self.count)]
        self.backward = [(order[p], order[(p - 1) % self.count]) for p in range(self.count)]
        position = [0] * self.count
        for p, member in enumerate(order):
            position[member] = p
        self.position = position

    def sources(self):
        me = jnp.asarray(self.position, jnp.int32)[lax.axis_index("fsdp")]
        steps = jnp.arange(self.count, dtype=jnp.int32)
        return jnp.asarray(self.order, jnp.int32)[(me - steps) % self.count]

    def chains(self, width, parts):
        cuts = [round(width * i / (2 * parts) / LANE) * LANE for i in range(2 * parts + 1)]
        cuts[-1] = width
        return [(cuts[i], cuts[i + 1], i % 2 == 0) for i in range(2 * parts)]

    def all_gather(self, local, core, side, core_pairs, parts):
        count = self.count
        mine_cols = lax.dynamic_slice_in_dim(local, core * side, side, axis=1)
        other_cols = lax.dynamic_slice_in_dim(local, (1 - core) * side, side, axis=1)
        mine_parts, other_parts = [], []
        for lo, hi, ahead in self.chains(side, parts):
            pairs = self.forward if ahead else self.backward
            piece = mine_cols[:, lo:hi]
            got, passed = [None] * count, [None] * count
            got[0], passed[0] = piece, other_cols[:, lo:hi]
            for step in range(1, count):
                piece = lax.ppermute(piece, "fsdp", pairs)
                k = step if ahead else count - step
                got[k] = piece
                passed[k] = lax.ppermute(piece, "dp", core_pairs)
            mine_parts.append(got)
            other_parts.append(passed)
        return mine_parts, other_parts

    def reduce_scatter(self, full, rows, outer_pairs, core_pairs, parts):
        count = self.count
        width = full.shape[1]
        outs, partners = [], []
        for lo, hi, ahead in self.chains(width, parts):
            pairs = self.forward if ahead else self.backward

            def block(k):
                return full[k * rows : (k + 1) * rows, lo:hi]

            acc = block(1 % count if ahead else count - 1)
            for step in range(1, count):
                got = lax.ppermute(acc.astype(jnp.bfloat16), "fsdp", pairs)
                k = (step + 1) % count if ahead else (count - step - 1) % count
                acc = got.astype(jnp.float32) + block(k)
            other = lax.ppermute(acc.astype(jnp.bfloat16), "dp", outer_pairs)
            acc = acc + other.astype(jnp.float32)
            outs.append(acc)
            partners.append(lax.ppermute(acc, "dp", core_pairs))
        return jnp.concatenate(outs, axis=1), jnp.concatenate(partners, axis=1)


def make_local(ring):
    def local(
        tokens,
        cotangent,
        masked_pos,
        labels,
        decoder,
        master,
        small_params,
        small_first,
        small_second,
        block_slots,
        first_moment,
        second_moment,
        left_bases,
        right_bases,
    ):
        model_width = decoder.shape[1]
        hidden = (master.shape[1] - 4 * model_width) // 2
        heads_count = model_width // HEAD_DIM
        token_count = tokens.shape[0]
        row_count, weight_cols = master.shape
        small_cols = small_params.shape[1]
        members = lax.axis_size("fsdp")
        core = lax.axis_index("dp") % 2
        replicas = lax.axis_size("dp")
        core_pairs = [(i, i ^ 1) for i in range(replicas)]
        outer_pairs = [(i, i ^ 2) for i in range(replicas)]
        half = weight_cols // 2
        lead = LANE
        side = half + lead
        split = (side // LANE + 1) // 2 * LANE

        sources = ring.sources()
        feature_of = (
            sources[:, None] * row_count + jnp.arange(row_count, dtype=jnp.int32)[None, :]
        ).reshape(-1)
        natural_of = jnp.zeros_like(feature_of).at[feature_of].set(
            jnp.arange(feature_of.shape[0], dtype=jnp.int32)
        )

        picker = (
            jnp.arange(model_width, dtype=jnp.int32)[:, None] == feature_of[None, :]
        ).astype(jnp.bfloat16)

        def to_rel(a):
            return jnp.dot(a, picker, preferred_element_type=jnp.float32).astype(a.dtype)

        def to_nat(a):
            return lax.dot_general(
                a, picker, (((1,), (1,)), ((), ())), precision=EXACT_PRECISION,
                preferred_element_type=jnp.float32,
            )

        w_low = master.astype(jnp.bfloat16)
        s_low = small_params.astype(jnp.bfloat16)
        packed_local = jnp.concatenate(
            [
                s_low,
                jnp.zeros((row_count, lead - small_cols), jnp.bfloat16),
                w_low,
                jnp.zeros((row_count, lead), jnp.bfloat16),
            ],
            axis=1,
        )
        mine, other = ring.all_gather(packed_local, core, side, core_pairs, 1)

        def assemble(first, second):
            return jnp.concatenate(
                [jnp.concatenate(chain, axis=0) for chain in first + second], axis=1
            )

        full = jnp.where(core == 0, assemble(mine, other), assemble(other, mine))
        weights = full[:, lead : lead + weight_cols]
        params = jnp.take(full[:, :small_cols].astype(jnp.float32), natural_of, axis=0)

        gain_one, shift_one, bias_query, bias_value, bias_output, gain_two, shift_two, bias_down = [
            params[:, column] for column in range(8)
        ]
        bias_up = params[:, 8:].reshape(hidden)
        rows_in = tokens.astype(jnp.float32)
        normed = normalize_layer(rows_in, gain_one, shift_one).astype(jnp.bfloat16)
        normed_rel = to_rel(normed)
        bias_qkv = jnp.concatenate([bias_query, jnp.zeros_like(bias_query), bias_value])
        projected = (
            jnp.dot(normed_rel, weights[:, : 3 * model_width], preferred_element_type=jnp.float32)
            + bias_qkv
        ).astype(jnp.bfloat16)
        seq_count = token_count // SEQ_LEN
        per_block = max(1, min(seq_count, 512 // SEQ_LEN))
        block_shape = (seq_count // per_block, per_block, SEQ_LEN, heads_count, HEAD_DIM)
        queries = projected[:, :model_width].reshape(block_shape)
        key_rows = projected[:, model_width : 2 * model_width].reshape(block_shape)
        values = projected[:, 2 * model_width :].reshape(block_shape)
        attention_result, log_total = lax.map(attend_block, (queries, key_rows, values))
        attention_result = attention_result.reshape(token_count, model_width)
        attended_rel = to_rel(attention_result)
        middle = (
            rows_in
            + jnp.dot(
                attended_rel,
                weights[:, 3 * model_width : 4 * model_width],
                preferred_element_type=jnp.float32,
            )
            + bias_output
        )
        normed_two = normalize_layer(middle, gain_two, shift_two).astype(jnp.bfloat16)
        normed_two_rel = to_rel(normed_two)
        pre_active = (
            jnp.dot(
                normed_two_rel,
                weights[:, 4 * model_width : 4 * model_width + hidden],
                preferred_element_type=jnp.float32,
            )
            + bias_up
        )
        active = exact_gelu(pre_active).astype(jnp.bfloat16)
        output_rows = (
            middle
            + to_nat(times_transpose(active, weights[:, 4 * model_width + hidden :]))
            + bias_down
        )
        out_tokens = output_rows.astype(jnp.bfloat16)
        logits = times_transpose(out_tokens, decoder)
        log_norm = jax.nn.logsumexp(logits, axis=-1)
        one_hot = (
            labels[:, None] == jnp.arange(decoder.shape[0], dtype=jnp.int32)[None, :]
        ).astype(jnp.float32)
        hidden_tokens = masked_pos.astype(jnp.float32)
        chosen = one_hot * hidden_tokens[:, None]
        entropy = log_norm - jnp.sum(one_hot * logits, axis=-1)
        right_prob = jnp.sum(one_hot * jnp.exp(logits - log_norm[:, None]), axis=-1)
        local_sums = jnp.concatenate(
            [jnp.sum(hidden_tokens * entropy)[None], jnp.sum(chosen * right_prob[:, None], axis=0)]
        )
        totals = jnp.concatenate([local_sums, jnp.sum(chosen, axis=0)])
        for axis in ("dp", "fsdp"):
            size = lax.axis_size(axis)
            reach = 1
            while reach < size:
                totals = totals + lax.ppermute(
                    totals, axis, [(i, i ^ reach) for i in range(size)]
                )
                reach *= 2
        global_sums, global_counts = totals[: local_sums.shape[0]], totals[local_sums.shape[0] :]
        loss_accuracy = jnp.concatenate(
            [
                global_sums[:1] / jnp.maximum(jnp.sum(global_counts), 1.0),
                global_sums[1:] / jnp.maximum(global_counts, 1.0),
            ]
        )
        counts = global_counts.astype(jnp.int32)
        back_rows = cotangent.astype(jnp.float32)
        cotangent_rel = to_rel(cotangent)
        d_active = jnp.dot(
            cotangent_rel, weights[:, 4 * model_width + hidden :], preferred_element_type=jnp.float32
        )
        unused, gelu_pull = jax.vjp(exact_gelu, pre_active)
        d_pre = gelu_pull(d_active)[0].astype(jnp.bfloat16)
        d_normed_two = to_nat(
            times_transpose(d_pre, weights[:, 4 * model_width : 4 * model_width + hidden])
        )
        unused, norm_pull_two = jax.vjp(normalize_layer, middle, params[:, 5], params[:, 6])
        d_middle_norm, d_gain_two, d_shift_two = norm_pull_two(d_normed_two)
        d_middle = back_rows + d_middle_norm
        d_branch = d_middle.astype(jnp.bfloat16)
        d_attended = to_nat(
            times_transpose(d_branch, weights[:, 3 * model_width : 4 * model_width])
        ).astype(jnp.bfloat16)
        d_queries, d_keys, d_values = lax.map(
            attend_back, (queries, key_rows, values, log_total, d_attended.reshape(block_shape))
        )
        d_projected = jnp.concatenate(
            [
                d_queries.reshape(token_count, model_width),
                d_keys.reshape(token_count, model_width),
                d_values.reshape(token_count, model_width),
            ],
            axis=1,
        )
        d_normed = to_nat(times_transpose(d_projected, weights[:, : 3 * model_width]))
        unused, norm_pull_one = jax.vjp(normalize_layer, rows_in, params[:, 0], params[:, 1])
        d_rows_norm, d_gain_one, d_shift_one = norm_pull_one(d_normed)
        grad_tokens = (d_middle + d_rows_norm).astype(jnp.bfloat16)
        proj_sums = jnp.sum(d_projected.astype(jnp.float32), axis=0)
        small_grads = jnp.stack(
            [
                d_gain_one,
                d_shift_one,
                proj_sums[:model_width],
                proj_sums[2 * model_width :],
                jnp.sum(d_branch.astype(jnp.float32), axis=0),
                d_gain_two,
                d_shift_two,
                jnp.sum(back_rows, axis=0),
            ],
            axis=1,
        )
        small_grads = jnp.concatenate(
            [small_grads, jnp.sum(d_pre.astype(jnp.float32), axis=0).reshape(model_width, -1)], axis=1
        )
        small_rel = jnp.take(small_grads, feature_of, axis=0)
        up_first = side - lead - 4 * model_width

        def halves(flip):
            def build():
                grad_up = contract_rows(normed_two_rel, d_pre)
                first = jnp.concatenate(
                    [
                        small_rel,
                        jnp.zeros((model_width, lead - small_cols), jnp.float32),
                        contract_rows(normed_rel, d_projected),
                        contract_rows(attended_rel, d_branch),
                        grad_up[:, :up_first],
                    ],
                    axis=1,
                )
                second = jnp.concatenate(
                    [
                        grad_up[:, up_first:],
                        contract_rows(cotangent_rel, active),
                        jnp.zeros((model_width, lead), jnp.float32),
                    ],
                    axis=1,
                )
                kept, given = (second, first) if flip else (first, second)
                return kept, given.astype(jnp.bfloat16)

            return build

        keep, send = lax.cond(core == 0, halves(False), halves(True))
        chip = keep + lax.ppermute(send, "dp", core_pairs).astype(jnp.float32)
        total, partner = ring.reduce_scatter(chip, row_count, outer_pairs, core_pairs, 2)
        joined = lax.cond(
            core == 0,
            lambda a, b: jnp.concatenate([a, b], axis=1),
            lambda a, b: jnp.concatenate([b, a], axis=1),
            total,
            partner,
        )
        grad_w = joined[:, lead : lead + weight_cols]
        grad_s = joined[:, :small_cols]

        block_width = model_width // 2
        block_count = grad_w.shape[1] // block_width
        owned_slots = first_moment.shape[0]
        devices = members
        slot_ids = jnp.arange(owned_slots * devices, dtype=jnp.int32)
        matches = block_slots[None, :] == slot_ids[:, None]
        in_use = jnp.any(matches, axis=1)
        source_block = jnp.sum(
            jnp.where(matches, jnp.arange(block_count, dtype=jnp.int32)[None, :], 0), axis=1
        )
        quarter = block_width // 2
        outgoing = jnp.take(grad_w.reshape(row_count, block_count, block_width), source_block, axis=1)
        outgoing = lax.dynamic_slice_in_dim(outgoing, core * quarter, quarter, axis=2)
        outgoing = jnp.where(in_use[None, :, None], outgoing, 0.0).reshape(
            row_count, devices, owned_slots, quarter
        )
        outgoing = jnp.transpose(outgoing, (2, 0, 1, 3)).astype(jnp.bfloat16)
        incoming = lax.all_to_all(
            outgoing, "fsdp", split_axis=2, concat_axis=1, tiled=True
        ).reshape(owned_slots, row_count * devices, quarter)
        incoming_other = lax.ppermute(incoming, "dp", core_pairs)
        incoming = lax.cond(
            core == 0,
            lambda: jnp.concatenate([incoming, incoming_other], axis=2),
            lambda: jnp.concatenate([incoming_other, incoming], axis=2),
        ).astype(jnp.float32)
        my_use = lax.dynamic_slice_in_dim(in_use, lax.axis_index("fsdp") * owned_slots, owned_slots)
        eigen_turned = jnp.einsum("kdi,kdc->kic", left_bases, incoming, precision=OPT_PRECISION)
        eigen_turned = jnp.einsum("kic,kcj->kij", eigen_turned, right_bases, precision=OPT_PRECISION)
        first_new = BETA_FIRST * first_moment + (1.0 - BETA_FIRST) * eigen_turned
        second_new = BETA_SECOND * second_moment + (1.0 - BETA_SECOND) * eigen_turned * eigen_turned
        direction = adam_direction(first_new, second_new)
        rotated_gradient = jnp.einsum("kij,klj->kil", direction, right_bases, precision=OPT_PRECISION)
        rotated_gradient = jnp.einsum(
            "kdi,kil->kdl", left_bases, rotated_gradient, precision=OPT_PRECISION
        )
        going = lax.dynamic_slice_in_dim(rotated_gradient, core * quarter, quarter, axis=2)
        returned = lax.all_to_all(
            going.reshape(owned_slots, devices, row_count, quarter).astype(jnp.bfloat16),
            "fsdp",
            split_axis=1,
            concat_axis=1,
            tiled=True,
        )
        returned_other = lax.ppermute(returned, "dp", core_pairs)
        returned_full = lax.cond(
            core == 0,
            lambda: jnp.concatenate([returned, returned_other], axis=3),
            lambda: jnp.concatenate([returned_other, returned], axis=3),
        ).reshape(owned_slots * devices, row_count, block_width)
        slot_row = (block_slots % owned_slots) * devices + block_slots // owned_slots
        update = jnp.take(returned_full, slot_row, axis=0).astype(jnp.float32)
        update = jnp.transpose(update, (1, 0, 2)).reshape(row_count, block_count * block_width)
        new_master = master - RATE_MATRIX * update
        new_copy = new_master.astype(jnp.bfloat16)
        keep_slot = my_use[:, None, None]
        new_first = jnp.where(keep_slot, first_new, 0.0)
        new_second = jnp.where(keep_slot, second_new, 0.0)
        new_small_first = BETA_FIRST * small_first + (1.0 - BETA_FIRST) * grad_s
        new_small_second = BETA_SECOND * small_second + (1.0 - BETA_SECOND) * grad_s * grad_s
        new_small = small_params - RATE_VECTOR * adam_direction(new_small_first, new_small_second)
        return (
            out_tokens,
            grad_tokens,
            grad_w,
            grad_s,
            new_first,
            new_second,
            new_master,
            new_copy,
            new_small,
            new_small_first,
            new_small_second,
            loss_accuracy,
            counts,
        )

    return local


def solution(mesh):
    members = mesh.devices[0]
    coords = [tuple(getattr(d, "coords", None) or ()) or None for d in members]
    ring = Ring(ring_order(coords))
    return jax.shard_map(
        make_local(ring),
        mesh=mesh,
        in_specs=(
            P(("dp", "fsdp"), None),
            P(("dp", "fsdp"), None),
            P(("dp", "fsdp")),
            P(("dp", "fsdp")),
            P(),
            P("fsdp", None),
            P("fsdp", None),
            P("fsdp", None),
            P("fsdp", None),
            P(),
            P("fsdp", None, None),
            P("fsdp", None, None),
            P("fsdp", None, None),
            P("fsdp", None, None),
        ),
        out_specs=(
            P(("dp", "fsdp"), None),
            P(("dp", "fsdp"), None),
            P("fsdp", None),
            P("fsdp", None),
            P("fsdp", None, None),
            P("fsdp", None, None),
            P("fsdp", None),
            P("fsdp", None),
            P("fsdp", None),
            P("fsdp", None),
            P("fsdp", None),
            P(),
            P(),
        ),
        check_vma=False,
    )
```
